32 devices in a mesh: parts: 2 (over x), chan: 8 (over z, y), samp: 2 (over core).
Axes of the slice: x: 2, y: 2, z: 4, core: 2. Of those that a mesh axis runs over, the one named last changes fastest.
Arguments:
- images: bfloat16 [512, 256, 784], P(('parts', 'samp'), 'chan'), parts along dimension 0, may hold values from -6 to 6
- out_grads: bfloat16 [512, 256, 196], P(('parts', 'samp'), 'chan'), parts along dimension 0, may hold values from -6 to 6
- in_signs: int32 [256, 288], P('chan'), may hold values from 0 to 1
- out_signs: int32 [256, 32], P('chan'), may hold values from 0 to 1
Outputs:
- sketch_rows: float32 [2, 256, 1024], P('samp', ('parts', 'chan')), parts along dimension 1
- r_factor: float32 [2048, 1024], P(('parts', 'chan')), parts along dimension 0
The draws below stay inside these ranges and needn't reach their ends.
There are 2 independent parts, one for each index of `parts`. The reference program is written for one: setup_inputs(seed, part) draws one part's arguments, and reference() takes and returns one part's arrays. A program takes and returns all parts, laid end to end along the dimension named above; an argument that names none is the same for every part. Nothing has to cross between parts.
All inputs are finite; a program needn't handle non-finite values.
Results may differ from the reference program's by a relative error of at most 0.0003.
Values sent between devices are 32-bit elements; how exact they have to be, the bound alone decides.
No kernel may reach another device: no remote copies, remote signals or barrier semaphores. Data moves between devices by JAX's collectives and lax.ppermute only.
A program may use at most 128 MiB of HBM per device.

```python
import math
import jax
import jax.numpy as jnp
from jax import lax

C = 256
K_IN = 32
K_OUT = 32
S_DEV = 128
HW_IN = 784
HW_OUT = 196
BATCH = 256
N_SAMP = 2


def set_ends(result, own_key, smallest, largest):
    index_at = [jax.random.randint(jax.random.fold_in(own_key, axis), (), 0, length) for axis, length in enumerate(result.shape)]
    longest = result.shape.index(max(result.shape))
    next_to = index_at[:longest] + [(index_at[longest] + 1) % result.shape[longest]] + index_at[longest + 1:]
    return result.at[tuple(index_at)].set(smallest).at[tuple(next_to)].set(largest)


def with_spikes(drawn, stream_key, source, target, parts, factor):
    owner, partner = [(jnp.arange(drawn.shape[dim]) // (drawn.shape[dim] // parts)).reshape([-1 if axis == dim else 1 for axis in range(drawn.ndim)]) for dim in (source, target)]
    chosen = jax.random.permutation(stream_key, parts)[partner]
    strong = (owner == chosen) | (owner == (partner + parts // 2) % parts)
    return jnp.where(strong, factor * drawn, drawn)


def block_scale(key, dims, split, low, high):
    def one(axis_at, blocks):
        steps = jax.random.uniform(jax.random.fold_in(jax.random.fold_in(key, 6), axis_at), (blocks,), jnp.float32, low / len(split), high / len(split))
        return jnp.repeat(jnp.exp(steps), dims[axis_at] // blocks).reshape((-1,) + (1,) * (len(dims) - axis_at - 1))

    loudness = one(*split[0])
    for cut in split[1:]:
        loudness = loudness * one(*cut)
    return loudness


def gaussian(rng, extent, deviation, limit, cuts=(), kind=jnp.bfloat16):
    array = deviation * jax.random.normal(rng, extent, jnp.float32)
    if cuts:
        array = array * block_scale(rng, extent, cuts, -0.22, 0.18)
    return jnp.clip(array, -limit, limit).astype(kind)


def bell_draw_with(own_key, dims, scale, most, pieces, heavy, kind=jnp.bfloat16):
    entries = scale * jax.random.normal(own_key, dims, jnp.float32)
    if pieces:
        entries = entries * block_scale(own_key, dims, pieces, -0.22, 0.18)
    return jnp.clip(with_spikes(entries, jax.random.fold_in(own_key, 3), *heavy), -most, most).astype(kind)


def setup_inputs(seed: int = 0, part: int = 0) -> dict:
    streams_of = jax.random.split(jax.random.key(seed), 5)
    part_splits = jax.random.split(jax.random.fold_in(streams_of[4], part), 5)
    images = bell_draw_with(part_splits[0], (BATCH, C, HW_IN), 1.0, 6.0, ((0, 2), (1, 8)), (1, 0, 8, 2.0))
    out_grads = gaussian(part_splits[1], (BATCH, C, HW_OUT), 1.0, 6.0, ((0, 2), (1, 8)))
    in_signs = set_ends(jax.random.randint(streams_of[2], (C, 9 * K_IN), 0, 2), jax.random.fold_in(streams_of[2], 1), 0, 1).astype(jnp.int32)
    out_signs = set_ends(jax.random.randint(streams_of[3], (C, K_OUT), 0, 2), jax.random.fold_in(streams_of[3], 1), 0, 1).astype(jnp.int32)
    return dict(images=images, out_grads=out_grads, in_signs=in_signs, out_signs=out_signs)


def project(images, out_grads, in_signs, out_signs):
    samples, channels, cells = images.shape
    side_in = math.isqrt(cells)
    side_out = side_in // 2
    picture = images.reshape(samples, channels, side_in, side_in)
    padded = jnp.pad(picture, ((0, 0), (0, 0), (1, 1), (1, 1)))
    tap_list = []
    for row_tap in range(3):
        for col_tap in range(3):
            tap_list.append(padded[:, :, row_tap:row_tap + 2 * side_out - 1:2, col_tap:col_tap + 2 * side_out - 1:2])
    patches = jnp.stack(tap_list, axis=2).reshape(samples, channels, 9, side_out * side_out)
    width_in = in_signs.shape[1] // 9
    in_matrix = (2 * in_signs - 1).astype(jnp.bfloat16).reshape(channels, 9, width_in)
    out_matrix = (2 * out_signs - 1).astype(jnp.bfloat16)
    in_part = jnp.einsum('nctp,ctj->njp', patches.astype(jnp.float32), in_matrix.astype(jnp.float32), preferred_element_type=jnp.float32)
    out_part = jnp.einsum('ncp,cl->nlp', out_grads.astype(jnp.float32), out_matrix.astype(jnp.float32), preferred_element_type=jnp.float32)
    return (in_part, out_part)

def sketch(in_sum, out_sum, total_channels):
    in_feat = in_sum / math.sqrt(9 * total_channels)
    out_feat = out_sum / math.sqrt(total_channels)
    cells = in_sum.shape[2]
    outer = jnp.einsum('nlp,njp->nlj', out_feat, in_feat, precision=lax.Precision.HIGHEST) / math.sqrt(cells)
    return outer.reshape(outer.shape[0], -1)

def reference(images, out_grads, in_signs, out_signs):

    def one_sample(pair):
        image_one, grad_one = pair
        in_part, out_part = project(image_one[None], grad_one[None], in_signs, out_signs)
        return sketch(in_part, out_part, C)[0]
    every = lax.map(one_sample, (images, out_grads))
    width = every.shape[1]
    gram_total = jnp.einsum('nk,nm->km', every, every, precision=lax.Precision.HIGHEST) / BATCH
    factor = jnp.linalg.cholesky(gram_total + jnp.eye(width, dtype=jnp.float32)).T
    return (every.reshape(N_SAMP, S_DEV, width), factor)
```

```python
import math

import jax
import jax.numpy as jnp
from jax import lax
from jax.sharding import PartitionSpec as P

C = 256


def project(images, out_grads, in_signs, out_signs):
    samples, channels, cells = images.shape
    side_in = math.isqrt(cells)
    picture = images.reshape(samples, channels, side_in, side_in)
    width_in = in_signs.shape[1] // 9
    in_matrix = (2 * in_signs - 1).astype(jnp.bfloat16).reshape(channels, 3, 3, width_in)
    kernel = jnp.transpose(in_matrix, (3, 0, 1, 2))
    in_part = lax.conv_general_dilated(
        picture,
        kernel,
        window_strides=(2, 2),
        padding=((1, 1), (1, 1)),
        dimension_numbers=("NCHW", "OIHW", "NCHW"),
        preferred_element_type=jnp.float32,
    )
    in_part = in_part.reshape(samples, width_in, -1)
    out_matrix = (2 * out_signs - 1).astype(jnp.bfloat16)
    out_part = jnp.einsum("ncp,cl->nlp", out_grads, out_matrix, preferred_element_type=jnp.float32)
    return (in_part, out_part)


def sketch(in_sum, out_sum, total_channels):
    in_feat = in_sum / math.sqrt(9 * total_channels)
    out_feat = out_sum / math.sqrt(total_channels)
    cells = in_sum.shape[2]
    outer = jnp.einsum(
        "nlp,njp->nlj", out_feat, in_feat, precision=lax.Precision.HIGHEST
    ) / math.sqrt(cells)
    return outer.reshape(outer.shape[0], -1)


def local(images, out_grads, in_signs, out_signs):
    samples = images.shape[0]
    in_part, out_part = project(images, out_grads, in_signs, out_signs)
    width_in = in_part.shape[1]
    both = jnp.concatenate([in_part, out_part], axis=1).reshape(samples, -1)
    both = lax.psum_scatter(both, "chan", scatter_dimension=0, tiled=True)
    both = both.reshape(both.shape[0], -1, in_part.shape[2])
    in_sum = both[:, :width_in]
    out_sum = both[:, width_in:]
    own = sketch(in_sum, out_sum, C)
    every = lax.all_gather(own, ("samp", "chan"), axis=0, tiled=True)
    batch_total = samples * lax.axis_size("samp")
    width = every.shape[1]
    identity_mat = jnp.eye(width, dtype=jnp.float32)
    gram = jnp.einsum("nk,nm->km", every, every, precision=lax.Precision.HIGHEST) / batch_total
    factor = jnp.linalg.cholesky(gram + identity_mat).T
    chan_count = lax.axis_size("chan")
    rows_here = width // chan_count
    r_rows = lax.dynamic_slice_in_dim(factor, lax.axis_index("chan") * rows_here, rows_here, 0)
    return (own[None], r_rows)


def solution(mesh):
    in_specs = (
        P(("parts", "samp"), "chan", None),
        P(("parts", "samp"), "chan", None),
        P("chan", None),
        P("chan", None),
    )
    out_specs = (P("samp", ("parts", "chan"), None), P(("parts", "chan"), None))
    return jax.shard_map(local, mesh=mesh, in_specs=in_specs, out_specs=out_specs, check_vma=False)
```

```python
import math

import jax
import jax.numpy as jnp
from jax import lax
from jax.experimental import pallas as pl
from jax.experimental.pallas import tpu as pltpu
from jax.sharding import PartitionSpec as P
import functools

C = 256
HI = lax.Precision.HIGHEST


def _factor_block(d, b):
    rows = lax.broadcasted_iota(jnp.int32, (b, 2 * b), 0)
    lanes = lax.broadcasted_iota(jnp.int32, (1, 2 * b), 1)
    x = jnp.concatenate([d, jnp.eye(b, dtype=jnp.float32)], axis=1)
    for j in range(b):
        row = x[j:j + 1, :]
        s = lax.rsqrt(row[:, j:j + 1])
        r = jnp.where(lanes >= j, row * s, 0.0)
        c = jnp.where(rows[:, :1] > j, x[:, j:j + 1] * s, 0.0)
        x = jnp.where(rows == j, r, x - c * r)
    return x[:, :b], x[:, b:]


def _chol_kernel(a_ref, r_ref, w_ref, *, nb, b):
    n = nb * b
    w_ref[...] = a_ref[...]

    def step(k, carry):
        wk = w_ref[k]
        d = jnp.zeros((b, b), jnp.float32)
        for j in range(nb):
            d = jnp.where(k == j, wk[:, j * b:(j + 1) * b], d)
        rkk, linv = _factor_block(d, b)
        pfull = jnp.dot(linv, wk, precision=HI, preferred_element_type=jnp.float32)
        blocks = []
        pblocks = []
        for j in range(nb):
            pj = pfull[:, j * b:(j + 1) * b]
            blocks.append(jnp.where(j > k, pj, jnp.where(j == k, rkk, 0.0)))
            pblocks.append(jnp.where(j > k, pj, 0.0))
        r_ref[k] = jnp.concatenate(blocks, axis=1)
        p = jnp.concatenate(pblocks, axis=1)
        for i in range(nb):
            @pl.when(i > k)
            def _():
                ti = pblocks[i]
                upd = lax.dot_general(ti, p, (((0,), (0,)), ((), ())), precision=HI,
                                      preferred_element_type=jnp.float32)
                w_ref[i] = w_ref[i] - upd
        return carry

    lax.fori_loop(0, nb, step, 0)


def cholesky_upper(a, b=128, interpret=False):
    n = a.shape[0]
    nb = n // b
    a3 = a.reshape(nb, b, n)
    out = pl.pallas_call(
        functools.partial(_chol_kernel, nb=nb, b=b),
        out_shape=jax.ShapeDtypeStruct((nb, b, n), jnp.float32),
        in_specs=[pl.BlockSpec(memory_space=pltpu.VMEM)],
        out_specs=pl.BlockSpec(memory_space=pltpu.VMEM),
        scratch_shapes=[pltpu.VMEM((nb, b, n), jnp.float32)],
        compiler_params=pltpu.CompilerParams(vmem_limit_bytes=48 * 1024 * 1024),
        interpret=interpret,
    )(a3)
    return out.reshape(n, n)


def project(images, out_grads, in_signs, out_signs):
    samples, channels, cells = images.shape
    side_in = math.isqrt(cells)
    picture = images.reshape(samples, channels, side_in, side_in)
    width_in = in_signs.shape[1] // 9
    in_matrix = (2 * in_signs - 1).astype(jnp.bfloat16).reshape(channels, 3, 3, width_in)
    kernel = jnp.transpose(in_matrix, (3, 0, 1, 2))
    in_part = lax.conv_general_dilated(
        picture,
        kernel,
        window_strides=(2, 2),
        padding=((1, 1), (1, 1)),
        dimension_numbers=("NCHW", "OIHW", "NCHW"),
        preferred_element_type=jnp.float32,
    )
    in_part = in_part.reshape(samples, width_in, -1)
    out_matrix = (2 * out_signs - 1).astype(jnp.bfloat16)
    out_part = jnp.einsum("ncp,cl->nlp", out_grads, out_matrix, preferred_element_type=jnp.float32)
    return (in_part, out_part)


def sketch(in_sum, out_sum, total_channels):
    in_feat = in_sum / math.sqrt(9 * total_channels)
    out_feat = out_sum / math.sqrt(total_channels)
    cells = in_sum.shape[2]
    outer = jnp.einsum(
        "nlp,njp->nlj", out_feat, in_feat, precision=lax.Precision.HIGHEST
    ) / math.sqrt(cells)
    return outer.reshape(outer.shape[0], -1)


def local(images, out_grads, in_signs, out_signs):
    samples = images.shape[0]
    in_part, out_part = project(images, out_grads, in_signs, out_signs)
    width_in = in_part.shape[1]
    both = jnp.concatenate([in_part, out_part], axis=1).reshape(samples, -1)
    both = lax.psum_scatter(both, "chan", scatter_dimension=0, tiled=True)
    both = both.reshape(both.shape[0], -1, in_part.shape[2])
    in_sum = both[:, :width_in]
    out_sum = both[:, width_in:]
    own = sketch(in_sum, out_sum, C)
    every = lax.all_gather(own, ("samp", "chan"), axis=0, tiled=True)
    batch_total = samples * lax.axis_size("samp")
    width = every.shape[1]
    identity_mat = jnp.eye(width, dtype=jnp.float32)
    gram = jnp.einsum("nk,nm->km", every, every, precision=lax.Precision.HIGHEST) / batch_total
    factor = cholesky_upper(gram + identity_mat)
    chan_count = lax.axis_size("chan")
    rows_here = width // chan_count
    r_rows = lax.dynamic_slice_in_dim(factor, lax.axis_index("chan") * rows_here, rows_here, 0)
    return (own[None], r_rows)


def solution(mesh):
    in_specs = (
        P(("parts", "samp"), "chan", None),
        P(("parts", "samp"), "chan", None),
        P("chan", None),
        P("chan", None),
    )
    out_specs = (P("samp", ("parts", "chan"), None), P(("parts", "chan"), None))
    return jax.shard_map(local, mesh=mesh, in_specs=in_specs, out_specs=out_specs, check_vma=False)
```

```python
import math

import jax
import jax.numpy as jnp
from jax import lax
from jax.experimental import pallas as pl
from jax.experimental.pallas import tpu as pltpu
from jax.sharding import PartitionSpec as P
import functools

C = 256
HI = lax.Precision.HIGHEST


def _factor_block(d, b):
    rows = lax.broadcasted_iota(jnp.int32, (b, 2 * b), 0)
    lanes = lax.broadcasted_iota(jnp.int32, (1, 2 * b), 1)
    x = jnp.concatenate([d, jnp.eye(b, dtype=jnp.float32)], axis=1)
    for j in range(b):
        row = x[j:j + 1, :]
        s = lax.rsqrt(row[:, j:j + 1])
        r = jnp.where(lanes >= j, row * s, 0.0)
        c = jnp.where(rows[:, :1] > j, x[:, j:j + 1] * s, 0.0)
        x = jnp.where(rows == j, r, x - c * r)
    return x[:, :b], x[:, b:]


def _chol_kernel(a_ref, r_ref, w_ref, *, nb, b):
    n = nb * b
    w_ref[...] = a_ref[...]

    def step(k, carry):
        wk = w_ref[k]
        d = jnp.zeros((b, b), jnp.float32)
        for j in range(nb):
            d = jnp.where(k == j, wk[:, j * b:(j + 1) * b], d)
        rkk, linv = _factor_block(d, b)
        pfull = jnp.dot(linv, wk, precision=HI, preferred_element_type=jnp.float32)
        blocks = []
        pblocks = []
        for j in range(nb):
            pj = pfull[:, j * b:(j + 1) * b]
            blocks.append(jnp.where(j > k, pj, jnp.where(j == k, rkk, 0.0)))
            pblocks.append(jnp.where(j > k, pj, 0.0))
        r_ref[k] = jnp.concatenate(blocks, axis=1)
        p = jnp.concatenate(pblocks, axis=1)
        for i in range(1, nb):
            @pl.when(i > k)
            def _():
                ti = pblocks[i]
                upd = lax.dot_general(ti, p[:, i * b:], (((0,), (0,)), ((), ())), precision=HI,
                                      preferred_element_type=jnp.float32)
                w_ref[i, :, i * b:] = w_ref[i, :, i * b:] - upd
        return carry

    lax.fori_loop(0, nb, step, 0)


def cholesky_upper(a, b=128, interpret=False):
    n = a.shape[0]
    nb = n // b
    a3 = a.reshape(nb, b, n)
    out = pl.pallas_call(
        functools.partial(_chol_kernel, nb=nb, b=b),
        out_shape=jax.ShapeDtypeStruct((nb, b, n), jnp.float32),
        in_specs=[pl.BlockSpec(memory_space=pltpu.VMEM)],
        out_specs=pl.BlockSpec(memory_space=pltpu.VMEM),
        scratch_shapes=[pltpu.VMEM((nb, b, n), jnp.float32)],
        compiler_params=pltpu.CompilerParams(vmem_limit_bytes=48 * 1024 * 1024),
        interpret=interpret,
    )(a3)
    return out.reshape(n, n)


def project(images, out_grads, in_signs, out_signs):
    samples, channels, cells = images.shape
    side_in = math.isqrt(cells)
    picture = images.reshape(samples, channels, side_in, side_in)
    width_in = in_signs.shape[1] // 9
    in_matrix = (2 * in_signs - 1).astype(jnp.bfloat16).reshape(channels, 3, 3, width_in)
    kernel = jnp.transpose(in_matrix, (3, 0, 1, 2))
    in_part = lax.conv_general_dilated(
        picture,
        kernel,
        window_strides=(2, 2),
        padding=((1, 1), (1, 1)),
        dimension_numbers=("NCHW", "OIHW", "NCHW"),
        preferred_element_type=jnp.float32,
    )
    in_part = in_part.reshape(samples, width_in, -1)
    out_matrix = (2 * out_signs - 1).astype(jnp.bfloat16)
    out_part = jnp.einsum("ncp,cl->nlp", out_grads, out_matrix, preferred_element_type=jnp.float32)
    return (in_part, out_part)


def sketch(in_sum, out_sum, total_channels):
    in_feat = in_sum / math.sqrt(9 * total_channels)
    out_feat = out_sum / math.sqrt(total_channels)
    cells = in_sum.shape[2]
    outer = jnp.einsum(
        "nlp,njp->nlj", out_feat, in_feat, precision=lax.Precision.HIGHEST
    ) / math.sqrt(cells)
    return outer.reshape(outer.shape[0], -1)


def local(images, out_grads, in_signs, out_signs):
    samples = images.shape[0]
    in_part, out_part = project(images, out_grads, in_signs, out_signs)
    width_in = in_part.shape[1]
    both = jnp.concatenate([in_part, out_part], axis=1).reshape(samples, -1)
    both = lax.psum_scatter(both, "chan", scatter_dimension=0, tiled=True)
    both = both.reshape(both.shape[0], -1, in_part.shape[2])
    in_sum = both[:, :width_in]
    out_sum = both[:, width_in:]
    own = sketch(in_sum, out_sum, C)
    every = lax.all_gather(own, ("samp", "chan"), axis=0, tiled=True)
    batch_total = samples * lax.axis_size("samp")
    width = every.shape[1]
    identity_mat = jnp.eye(width, dtype=jnp.float32)
    gram = jnp.einsum("nk,nm->km", every, every, precision=lax.Precision.HIGHEST) / batch_total
    factor = cholesky_upper(gram + identity_mat)
    chan_count = lax.axis_size("chan")
    rows_here = width // chan_count
    r_rows = lax.dynamic_slice_in_dim(factor, lax.axis_index("chan") * rows_here, rows_here, 0)
    return (own[None], r_rows)


def solution(mesh):
    in_specs = (
        P(("parts", "samp"), "chan", None),
        P(("parts", "samp"), "chan", None),
        P("chan", None),
        P("chan", None),
    )
    out_specs = (P("samp", ("parts", "chan"), None), P(("parts", "chan"), None))
    return jax.shard_map(local, mesh=mesh, in_specs=in_specs, out_specs=out_specs, check_vma=False)
```

```python
import math

import jax
import jax.numpy as jnp
from jax import lax
from jax.experimental import pallas as pl
from jax.experimental.pallas import tpu as pltpu
from jax.sharding import PartitionSpec as P
import functools

C = 256
HI = lax.Precision.HIGHEST


def _factor_block(d, b):
    rows = lax.broadcasted_iota(jnp.int32, (b, 2 * b), 0)
    lanes = lax.broadcasted_iota(jnp.int32, (1, 2 * b), 1)
    x = jnp.concatenate([d, jnp.eye(b, dtype=jnp.float32)], axis=1)
    for j in range(b):
        row = x[j:j + 1, :]
        s = lax.rsqrt(row[:, j:j + 1])
        r = jnp.where(lanes >= j, row * s, 0.0)
        c = jnp.where(rows[:, :1] > j, x[:, j:j + 1] * s, 0.0)
        x = jnp.where(rows == j, r, x - c * r)
    return x[:, :b], x[:, b:]


def _chol_kernel(a_ref, r_ref, w_ref, *, nb, b):
    n = nb * b
    w_ref[...] = a_ref[...]

    def step(k, carry):
        wk = w_ref[k]
        d = jnp.zeros((b, b), jnp.float32)
        for j in range(nb):
            d = jnp.where(k == j, wk[:, j * b:(j + 1) * b], d)
        rkk, linv = _factor_block(d, b)
        pfull = jnp.dot(linv, wk, precision=HI, preferred_element_type=jnp.float32)
        blocks = []
        pblocks = []
        for j in range(nb):
            pj = pfull[:, j * b:(j + 1) * b]
            blocks.append(jnp.where(j > k, pj, jnp.where(j == k, rkk, 0.0)))
            pblocks.append(jnp.where(j > k, pj, 0.0))
        r_ref[k] = jnp.concatenate(blocks, axis=1)
        p = jnp.concatenate(pblocks, axis=1)
        for i in range(1, nb):
            @pl.when(i > k)
            def _():
                ti = pblocks[i]
                upd = lax.dot_general(ti, p[:, i * b:], (((0,), (0,)), ((), ())), precision=HI,
                                      preferred_element_type=jnp.float32)
                w_ref[i, :, i * b:] = w_ref[i, :, i * b:] - upd
        return carry

    lax.fori_loop(0, nb, step, 0)


def cholesky_upper(a, b=128, interpret=False):
    n = a.shape[0]
    nb = n // b
    a3 = a.reshape(nb, b, n)
    out = pl.pallas_call(
        functools.partial(_chol_kernel, nb=nb, b=b),
        out_shape=jax.ShapeDtypeStruct((nb, b, n), jnp.float32),
        in_specs=[pl.BlockSpec(memory_space=pltpu.VMEM)],
        out_specs=pl.BlockSpec(memory_space=pltpu.VMEM),
        scratch_shapes=[pltpu.VMEM((nb, b, n), jnp.float32)],
        compiler_params=pltpu.CompilerParams(vmem_limit_bytes=48 * 1024 * 1024),
        interpret=interpret,
    )(a3)
    return out.reshape(n, n)


def project(images, out_grads, in_signs, out_signs):
    samples, channels, cells = images.shape
    side_in = math.isqrt(cells)
    picture = images.reshape(samples, channels, side_in, side_in)
    width_in = in_signs.shape[1] // 9
    in_matrix = (2 * in_signs - 1).astype(jnp.bfloat16).reshape(channels, 3, 3, width_in)
    kernel = jnp.transpose(in_matrix, (3, 0, 1, 2))
    in_part = lax.conv_general_dilated(
        picture,
        kernel,
        window_strides=(2, 2),
        padding=((1, 1), (1, 1)),
        dimension_numbers=("NCHW", "OIHW", "NCHW"),
        preferred_element_type=jnp.float32,
    )
    in_part = in_part.reshape(samples, width_in, -1)
    out_matrix = (2 * out_signs - 1).astype(jnp.bfloat16)
    out_part = jnp.einsum("ncp,cl->nlp", out_grads, out_matrix, preferred_element_type=jnp.float32)
    return (in_part, out_part)


def sketch(in_sum, out_sum, total_channels):
    in_feat = in_sum / math.sqrt(9 * total_channels)
    out_feat = out_sum / math.sqrt(total_channels)
    cells = in_sum.shape[2]
    outer = jnp.einsum(
        "nlp,njp->nlj", out_feat, in_feat, precision=lax.Precision.HIGHEST
    ) / math.sqrt(cells)
    return outer.reshape(outer.shape[0], -1)


def _ring_order(n):
    if n % 2:
        return list(range(n))
    return list(range(0, n, 2)) + list(range(n - 1, 0, -2))


def ring_reduce_scatter(x, axis):
    n = lax.axis_size(axis)
    order = _ring_order(n)
    pos = jnp.asarray([order.index(c) for c in range(n)], jnp.int32)[lax.axis_index(axis)]
    owner = jnp.asarray(order, jnp.int32)
    blocks = x.reshape(n, -1, x.shape[-1])
    h = x.shape[-1] // 2
    fwd = [(order[q], order[(q + 1) % n]) for q in range(n)]
    bwd = [(order[(q + 1) % n], order[q]) for q in range(n)]

    def take(q, lo, hi):
        blk = lax.dynamic_index_in_dim(blocks, owner[q % n], 0, keepdims=False)
        return blk[:, lo:hi]

    fa = take(pos - 1 + n, 0, h)
    ba = take(pos + 1, h, x.shape[-1])
    for step in range(1, n):
        fa = lax.ppermute(fa, axis, fwd) + take(pos - 1 - step + 2 * n, 0, h)
        ba = lax.ppermute(ba, axis, bwd) + take(pos + 1 + step, h, x.shape[-1])
    return jnp.concatenate([fa, ba], axis=-1)


def local(images, out_grads, in_signs, out_signs):
    samples = images.shape[0]
    in_part, out_part = project(images, out_grads, in_signs, out_signs)
    width_in = in_part.shape[1]
    both = jnp.concatenate([in_part, out_part], axis=1).reshape(samples, -1)
    both = ring_reduce_scatter(both, "chan")
    both = both.reshape(both.shape[0], -1, in_part.shape[2])
    in_sum = both[:, :width_in]
    out_sum = both[:, width_in:]
    own = sketch(in_sum, out_sum, C)
    every = lax.all_gather(own, ("samp", "chan"), axis=0, tiled=True)
    batch_total = samples * lax.axis_size("samp")
    width = every.shape[1]
    identity_mat = jnp.eye(width, dtype=jnp.float32)
    gram = jnp.einsum("nk,nm->km", every, every, precision=lax.Precision.HIGHEST) / batch_total
    factor = cholesky_upper(gram + identity_mat)
    chan_count = lax.axis_size("chan")
    rows_here = width // chan_count
    r_rows = lax.dynamic_slice_in_dim(factor, lax.axis_index("chan") * rows_here, rows_here, 0)
    return (own[None], r_rows)


def solution(mesh):
    in_specs = (
        P(("parts", "samp"), "chan", None),
        P(("parts", "samp"), "chan", None),
        P("chan", None),
        P("chan", None),
    )
    out_specs = (P("samp", ("parts", "chan"), None), P(("parts", "chan"), None))
    return jax.shard_map(local, mesh=mesh, in_specs=in_specs, out_specs=out_specs, check_vma=False)
```

```python
import math

import jax
import jax.numpy as jnp
from jax import lax
from jax.experimental import pallas as pl
from jax.experimental.pallas import tpu as pltpu
from jax.sharding import PartitionSpec as P
import functools

C = 256
HI = lax.Precision.HIGHEST


def _factor_block(d, b):
    rows = lax.broadcasted_iota(jnp.int32, (b, 2 * b), 0)
    lanes = lax.broadcasted_iota(jnp.int32, (1, 2 * b), 1)
    x = jnp.concatenate([d, jnp.eye(b, dtype=jnp.float32)], axis=1)
    for j in range(b):
        row = x[j:j + 1, :]
        s = lax.rsqrt(row[:, j:j + 1])
        r = jnp.where(lanes >= j, row * s, 0.0)
        c = jnp.where(rows[:, :1] > j, x[:, j:j + 1] * s, 0.0)
        x = jnp.where(rows == j, r, x - c * r)
    return x[:, :b], x[:, b:]


def _chol_kernel(a_ref, r_ref, w_ref, *, nb, b):
    n = nb * b
    w_ref[...] = a_ref[...]

    def step(k, carry):
        wk = w_ref[k]
        d = jnp.zeros((b, b), jnp.float32)
        for j in range(nb):
            d = jnp.where(k == j, wk[:, j * b:(j + 1) * b], d)
        rkk, linv = _factor_block(d, b)
        pfull = jnp.dot(linv, wk, precision=HI, preferred_element_type=jnp.float32)
        blocks = []
        pblocks = []
        for j in range(nb):
            pj = pfull[:, j * b:(j + 1) * b]
            blocks.append(jnp.where(j > k, pj, jnp.where(j == k, rkk, 0.0)))
            pblocks.append(jnp.where(j > k, pj, 0.0))
        r_ref[k] = jnp.concatenate(blocks, axis=1)
        p = jnp.concatenate(pblocks, axis=1)
        for i in range(1, nb):
            @pl.when(i > k)
            def _():
                ti = pblocks[i]
                upd = lax.dot_general(ti, p[:, i * b:], (((0,), (0,)), ((), ())), precision=HI,
                                      preferred_element_type=jnp.float32)
                w_ref[i, :, i * b:] = w_ref[i, :, i * b:] - upd
        return carry

    lax.fori_loop(0, nb, step, 0)


def cholesky_upper(a, b=128, interpret=False):
    n = a.shape[0]
    nb = n // b
    a3 = a.reshape(nb, b, n)
    out = pl.pallas_call(
        functools.partial(_chol_kernel, nb=nb, b=b),
        out_shape=jax.ShapeDtypeStruct((nb, b, n), jnp.float32),
        in_specs=[pl.BlockSpec(memory_space=pltpu.VMEM)],
        out_specs=pl.BlockSpec(memory_space=pltpu.VMEM),
        scratch_shapes=[pltpu.VMEM((nb, b, n), jnp.float32)],
        compiler_params=pltpu.CompilerParams(vmem_limit_bytes=48 * 1024 * 1024),
        interpret=interpret,
    )(a3)
    return out.reshape(n, n)


def project(images, out_grads, in_signs, out_signs):
    samples, channels, cells = images.shape
    side_in = math.isqrt(cells)
    picture = images.reshape(samples, channels, side_in, side_in)
    width_in = in_signs.shape[1] // 9
    in_matrix = (2 * in_signs - 1).astype(jnp.bfloat16).reshape(channels, 3, 3, width_in)
    kernel = jnp.transpose(in_matrix, (3, 0, 1, 2))
    in_part = lax.conv_general_dilated(
        picture,
        kernel,
        window_strides=(2, 2),
        padding=((1, 1), (1, 1)),
        dimension_numbers=("NCHW", "OIHW", "NCHW"),
        preferred_element_type=jnp.float32,
    )
    in_part = in_part.reshape(samples, width_in, -1)
    out_matrix = (2 * out_signs - 1).astype(jnp.bfloat16)
    out_part = jnp.einsum("ncp,cl->nlp", out_grads, out_matrix, preferred_element_type=jnp.float32)
    return (in_part, out_part)


def sketch(in_sum, out_sum, total_channels):
    in_feat = in_sum / math.sqrt(9 * total_channels)
    out_feat = out_sum / math.sqrt(total_channels)
    cells = in_sum.shape[2]
    outer = jnp.einsum(
        "nlp,njp->nlj", out_feat, in_feat, precision=lax.Precision.HIGHEST
    ) / math.sqrt(cells)
    return outer.reshape(outer.shape[0], -1)


def _ring_order(n):
    if n % 2:
        return list(range(n))
    return list(range(0, n, 2)) + list(range(n - 1, 0, -2))


def ring_reduce_scatter(x, axis, pair):
    n = lax.axis_size(axis)
    order = _ring_order(n)
    me = lax.axis_index(pair)
    pos = jnp.asarray([order.index(c) for c in range(n)], jnp.int32)[lax.axis_index(axis)]
    owner = jnp.asarray(order, jnp.int32)
    h = x.shape[-1] // 2
    swap = [(0, 1), (1, 0)]
    keep = jnp.where(me == 0, x[:, :h], x[:, h:])
    give = jnp.where(me == 0, x[:, h:], x[:, :h])
    both = jnp.stack([keep, lax.ppermute(give, pair, swap)])
    blocks = both.reshape(2, n, -1, h)
    ring = []
    for q in range(n):
        ring.append((order[q] * 2, order[(q + 1) % n] * 2))
        ring.append((order[(q + 1) % n] * 2 + 1, order[q] * 2 + 1))
    sign = 1 - 2 * me

    def take(step):
        q = (pos - sign * (1 + step) + 2 * n) % n
        return lax.dynamic_index_in_dim(blocks, owner[q], 1, keepdims=False)

    acc = take(0)
    for step in range(1, n):
        acc = lax.ppermute(acc, (axis, pair), ring) + take(step)
    back = lax.ppermute(acc[1], pair, swap)
    return jnp.where(me == 0, jnp.concatenate([acc[0], back], axis=-1),
                     jnp.concatenate([back, acc[0]], axis=-1))


def local(images, out_grads, in_signs, out_signs):
    samples = images.shape[0]
    in_part, out_part = project(images, out_grads, in_signs, out_signs)
    width_in = in_part.shape[1]
    both = jnp.concatenate([in_part, out_part], axis=1).reshape(samples, -1)
    both = ring_reduce_scatter(both, "chan", "samp")
    both = both.reshape(both.shape[0], -1, in_part.shape[2])
    in_sum = both[:, :width_in]
    out_sum = both[:, width_in:]
    own = sketch(in_sum, out_sum, C)
    every = lax.all_gather(own, ("samp", "chan"), axis=0, tiled=True)
    batch_total = samples * lax.axis_size("samp")
    width = every.shape[1]
    identity_mat = jnp.eye(width, dtype=jnp.float32)
    gram = jnp.einsum("nk,nm->km", every, every, precision=lax.Precision.HIGHEST) / batch_total
    factor = cholesky_upper(gram + identity_mat)
    chan_count = lax.axis_size("chan")
    rows_here = width // chan_count
    r_rows = lax.dynamic_slice_in_dim(factor, lax.axis_index("chan") * rows_here, rows_here, 0)
    return (own[None], r_rows)


def solution(mesh):
    in_specs = (
        P(("parts", "samp"), "chan", None),
        P(("parts", "samp"), "chan", None),
        P("chan", None),
        P("chan", None),
    )
    out_specs = (P("samp", ("parts", "chan"), None), P(("parts", "chan"), None))
    return jax.shard_map(local, mesh=mesh, in_specs=in_specs, out_specs=out_specs, check_vma=False)
```

```python
import math

import jax
import jax.numpy as jnp
from jax import lax
from jax.experimental import pallas as pl
from jax.experimental.pallas import tpu as pltpu
from jax.sharding import PartitionSpec as P
import functools

C = 256
HI = lax.Precision.HIGHEST


def _factor_block(d, b):
    rows = lax.broadcasted_iota(jnp.int32, (b, 2 * b), 0)
    lanes = lax.broadcasted_iota(jnp.int32, (1, 2 * b), 1)
    x = jnp.concatenate([d, jnp.eye(b, dtype=jnp.float32)], axis=1)
    for j in range(b):
        row = x[j:j + 1, :]
        s = lax.rsqrt(row[:, j:j + 1])
        r = jnp.where(lanes >= j, row * s, 0.0)
        c = jnp.where(rows[:, :1] > j, x[:, j:j + 1] * s, 0.0)
        x = jnp.where(rows == j, r, x - c * r)
    return x[:, :b], x[:, b:]


def _chol_kernel(a_ref, r_ref, w_ref, *, nb, b):
    n = nb * b
    w_ref[...] = a_ref[...]

    def step(k, carry):
        wk = w_ref[k]
        d = jnp.zeros((b, b), jnp.float32)
        for j in range(nb):
            d = jnp.where(k == j, wk[:, j * b:(j + 1) * b], d)
        rkk, linv = _factor_block(d, b)
        pfull = jnp.dot(linv, wk, precision=HI, preferred_element_type=jnp.float32)
        blocks = []
        pblocks = []
        for j in range(nb):
            pj = pfull[:, j * b:(j + 1) * b]
            blocks.append(jnp.where(j > k, pj, jnp.where(j == k, rkk, 0.0)))
            pblocks.append(jnp.where(j > k, pj, 0.0))
        r_ref[k] = jnp.concatenate(blocks, axis=1)
        p = jnp.concatenate(pblocks, axis=1)
        for i in range(1, nb):
            @pl.when(i > k)
            def _():
                ti = pblocks[i]
                upd = lax.dot_general(ti, p[:, i * b:], (((0,), (0,)), ((), ())), precision=HI,
                                      preferred_element_type=jnp.float32)
                w_ref[i, :, i * b:] = w_ref[i, :, i * b:] - upd
        return carry

    lax.fori_loop(0, nb, step, 0)


def cholesky_upper(a, b=128, interpret=False):
    n = a.shape[0]
    nb = n // b
    a3 = a.reshape(nb, b, n)
    out = pl.pallas_call(
        functools.partial(_chol_kernel, nb=nb, b=b),
        out_shape=jax.ShapeDtypeStruct((nb, b, n), jnp.float32),
        in_specs=[pl.BlockSpec(memory_space=pltpu.VMEM)],
        out_specs=pl.BlockSpec(memory_space=pltpu.VMEM),
        scratch_shapes=[pltpu.VMEM((nb, b, n), jnp.float32)],
        compiler_params=pltpu.CompilerParams(vmem_limit_bytes=48 * 1024 * 1024),
        interpret=interpret,
    )(a3)
    return out.reshape(n, n)


def project(images, out_grads, in_signs, out_signs):
    samples, channels, cells = images.shape
    side_in = math.isqrt(cells)
    picture = images.reshape(samples, channels, side_in, side_in)
    width_in = in_signs.shape[1] // 9
    in_matrix = (2 * in_signs - 1).astype(jnp.bfloat16).reshape(channels, 3, 3, width_in)
    kernel = jnp.transpose(in_matrix, (3, 0, 1, 2))
    in_part = lax.conv_general_dilated(
        picture,
        kernel,
        window_strides=(2, 2),
        padding=((1, 1), (1, 1)),
        dimension_numbers=("NCHW", "OIHW", "NCHW"),
        preferred_element_type=jnp.float32,
    )
    in_part = in_part.reshape(samples, width_in, -1)
    out_matrix = (2 * out_signs - 1).astype(jnp.bfloat16)
    out_part = jnp.einsum("ncp,cl->nlp", out_grads, out_matrix, preferred_element_type=jnp.float32)
    return (in_part, out_part)


def sketch(in_sum, out_sum, total_channels):
    in_feat = in_sum / math.sqrt(9 * total_channels)
    out_feat = out_sum / math.sqrt(total_channels)
    cells = in_sum.shape[2]
    outer = jnp.einsum(
        "nlp,njp->nlj", out_feat, in_feat, precision=lax.Precision.HIGHEST
    ) / math.sqrt(cells)
    return outer.reshape(outer.shape[0], -1)


def _ring_order(n):
    if n % 2:
        return list(range(n))
    return list(range(0, n, 2)) + list(range(n - 1, 0, -2))


def ring_reduce_scatter(x, axis, pair):
    n = lax.axis_size(axis)
    order = _ring_order(n)
    me = lax.axis_index(pair)
    pos = jnp.asarray([order.index(c) for c in range(n)], jnp.int32)[lax.axis_index(axis)]
    owner = jnp.asarray(order, jnp.int32)
    blocks = x.reshape(n, -1, x.shape[-1])
    ring = []
    for q in range(n):
        ring.append((order[q] * 2, order[(q + 1) % n] * 2))
        ring.append((order[(q + 1) % n] * 2 + 1, order[q] * 2 + 1))
    sign = 1 - 2 * me

    def take(step):
        q = (pos - sign * (1 + step) + 2 * n) % n
        return lax.dynamic_index_in_dim(blocks, owner[q], 0, keepdims=False)

    acc = take(0)
    for step in range(1, n):
        acc = lax.ppermute(acc, (axis, pair), ring) + take(step)
    return acc


def local(images, out_grads, in_signs, out_signs):
    samples = images.shape[0]
    in_part, out_part = project(images, out_grads, in_signs, out_signs)
    width_in = in_part.shape[1]
    both = jnp.concatenate([in_part, out_part], axis=1).reshape(samples, -1)
    both = ring_reduce_scatter(both, "chan", "samp")
    both = both.reshape(both.shape[0], -1, in_part.shape[2])
    in_sum = both[:, :width_in]
    out_sum = both[:, width_in:]
    own = sketch(in_sum, out_sum, C)
    every = lax.all_gather(own, ("samp", "chan"), axis=0, tiled=True)
    batch_total = samples * lax.axis_size("samp")
    width = every.shape[1]
    identity_mat = jnp.eye(width, dtype=jnp.float32)
    gram = jnp.einsum("nk,nm->km", every, every, precision=lax.Precision.HIGHEST) / batch_total
    factor = cholesky_upper(gram + identity_mat)
    chan_count = lax.axis_size("chan")
    rows_here = width // chan_count
    r_rows = lax.dynamic_slice_in_dim(factor, lax.axis_index("chan") * rows_here, rows_here, 0)
    return (own[None], r_rows)


def solution(mesh):
    in_specs = (
        P(("parts", "samp"), "chan", None),
        P(("parts", "samp"), "chan", None),
        P("chan", None),
        P("chan", None),
    )
    out_specs = (P("samp", ("parts", "chan"), None), P(("parts", "chan"), None))
    return jax.shard_map(local, mesh=mesh, in_specs=in_specs, out_specs=out_specs, check_vma=False)
```

```python
import math

import jax
import jax.numpy as jnp
from jax import lax
from jax.experimental import pallas as pl
from jax.experimental.pallas import tpu as pltpu
from jax.sharding import PartitionSpec as P
import functools

C = 256
HI = lax.Precision.HIGHEST


def _factor_block(d, b):
    rows = lax.broadcasted_iota(jnp.int32, (b, 2 * b), 0)
    lanes = lax.broadcasted_iota(jnp.int32, (1, 2 * b), 1)
    x = jnp.concatenate([d, jnp.eye(b, dtype=jnp.float32)], axis=1)
    for j in range(b):
        row = x[j:j + 1, :]
        s = lax.rsqrt(row[:, j:j + 1])
        r = jnp.where(lanes >= j, row * s, 0.0)
        c = jnp.where(rows[:, :1] > j, x[:, j:j + 1] * s, 0.0)
        x = jnp.where(rows == j, r, x - c * r)
    return x[:, :b], x[:, b:]


def _chol_kernel(a_ref, r_ref, w_ref, *, nb, b):
    n = nb * b
    w_ref[...] = a_ref[...]

    def step(k, carry):
        wk = w_ref[k]
        d = jnp.zeros((b, b), jnp.float32)
        for j in range(nb):
            d = jnp.where(k == j, wk[:, j * b:(j + 1) * b], d)
        rkk, linv = _factor_block(d, b)
        pfull = jnp.dot(linv, wk, precision=HI, preferred_element_type=jnp.float32)
        blocks = []
        pblocks = []
        for j in range(nb):
            pj = pfull[:, j * b:(j + 1) * b]
            blocks.append(jnp.where(j > k, pj, jnp.where(j == k, rkk, 0.0)))
            pblocks.append(jnp.where(j > k, pj, 0.0))
        r_ref[k] = jnp.concatenate(blocks, axis=1)
        p = jnp.concatenate(pblocks, axis=1)
        for i in range(1, nb):
            @pl.when(i > k)
            def _():
                ti = pblocks[i]
                upd = lax.dot_general(ti, p[:, i * b:], (((0,), (0,)), ((), ())), precision=HI,
                                      preferred_element_type=jnp.float32)
                w_ref[i, :, i * b:] = w_ref[i, :, i * b:] - upd
        return carry

    lax.fori_loop(0, nb, step, 0)


def cholesky_upper(a, b=128, interpret=False):
    n = a.shape[0]
    nb = n // b
    a3 = a.reshape(nb, b, n)
    out = pl.pallas_call(
        functools.partial(_chol_kernel, nb=nb, b=b),
        out_shape=jax.ShapeDtypeStruct((nb, b, n), jnp.float32),
        in_specs=[pl.BlockSpec(memory_space=pltpu.VMEM)],
        out_specs=pl.BlockSpec(memory_space=pltpu.VMEM),
        scratch_shapes=[pltpu.VMEM((nb, b, n), jnp.float32)],
        compiler_params=pltpu.CompilerParams(vmem_limit_bytes=48 * 1024 * 1024),
        interpret=interpret,
    )(a3)
    return out.reshape(n, n)


def project(images, out_grads, in_signs, out_signs):
    samples, channels, cells = images.shape
    side_in = math.isqrt(cells)
    picture = images.reshape(samples, channels, side_in, side_in)
    width_in = in_signs.shape[1] // 9
    in_matrix = (2 * in_signs - 1).astype(jnp.bfloat16).reshape(channels, 3, 3, width_in)
    kernel = jnp.transpose(in_matrix, (3, 0, 1, 2))
    in_part = lax.conv_general_dilated(
        picture,
        kernel,
        window_strides=(2, 2),
        padding=((1, 1), (1, 1)),
        dimension_numbers=("NCHW", "OIHW", "NCHW"),
        preferred_element_type=jnp.float32,
    )
    in_part = in_part.reshape(samples, width_in, -1)
    out_matrix = (2 * out_signs - 1).astype(jnp.bfloat16)
    out_part = jnp.einsum("ncp,cl->nlp", out_grads, out_matrix, preferred_element_type=jnp.float32)
    return (in_part, out_part)


def sketch(in_sum, out_sum, total_channels):
    in_feat = in_sum / math.sqrt(9 * total_channels)
    out_feat = out_sum / math.sqrt(total_channels)
    cells = in_sum.shape[2]
    outer = jnp.einsum(
        "nlp,njp->nlj", out_feat, in_feat, precision=lax.Precision.HIGHEST
    ) / math.sqrt(cells)
    return outer.reshape(outer.shape[0], -1)


def _ring_order(n):
    if n % 2:
        return list(range(n))
    return list(range(0, n, 2)) + list(range(n - 1, 0, -2))


def ring_reduce_scatter(x, axis, pair):
    n = lax.axis_size(axis)
    order = _ring_order(n)
    me = lax.axis_index(pair)
    pos = jnp.asarray([order.index(c) for c in range(n)], jnp.int32)[lax.axis_index(axis)]
    owner = jnp.asarray(order, jnp.int32)
    blocks = x.reshape(n, -1, x.shape[-1])
    ring = []
    for q in range(n):
        ring.append((order[q] * 2, order[(q + 1) % n] * 2))
        ring.append((order[(q + 1) % n] * 2 + 1, order[q] * 2 + 1))
    sign = 1 - 2 * me

    def take(step):
        q = (pos - sign * (1 + step) + 2 * n) % n
        return lax.dynamic_index_in_dim(blocks, owner[q], 0, keepdims=False)

    acc = take(0)
    for step in range(1, n):
        acc = lax.ppermute(acc, (axis, pair), ring) + take(step)
    return acc


def doubling_gather(x, axes):
    size = 1
    for a in axes:
        size *= lax.axis_size(a)
    if size & (size - 1):
        return lax.all_gather(x, axes, axis=0, tiled=True)
    k = 1
    while k < size:
        other = lax.ppermute(x, axes, [(i, i ^ k) for i in range(size)])
        x = jnp.concatenate([x, other], axis=0)
        k *= 2
    return x


def local(images, out_grads, in_signs, out_signs):
    samples = images.shape[0]
    in_part, out_part = project(images, out_grads, in_signs, out_signs)
    width_in = in_part.shape[1]
    both = jnp.concatenate([in_part, out_part], axis=1).reshape(samples, -1)
    both = ring_reduce_scatter(both, "chan", "samp")
    both = both.reshape(both.shape[0], -1, in_part.shape[2])
    in_sum = both[:, :width_in]
    out_sum = both[:, width_in:]
    own = sketch(in_sum, out_sum, C)
    every = doubling_gather(own, ("chan", "samp"))
    batch_total = samples * lax.axis_size("samp")
    width = every.shape[1]
    identity_mat = jnp.eye(width, dtype=jnp.float32)
    gram = jnp.einsum("nk,nm->km", every, every, precision=lax.Precision.HIGHEST) / batch_total
    factor = cholesky_upper(gram + identity_mat)
    chan_count = lax.axis_size("chan")
    rows_here = width // chan_count
    r_rows = lax.dynamic_slice_in_dim(factor, lax.axis_index("chan") * rows_here, rows_here, 0)
    return (own[None], r_rows)


def solution(mesh):
    in_specs = (
        P(("parts", "samp"), "chan", None),
        P(("parts", "samp"), "chan", None),
        P("chan", None),
        P("chan", None),
    )
    out_specs = (P("samp", ("parts", "chan"), None), P(("parts", "chan"), None))
    return jax.shard_map(local, mesh=mesh, in_specs=in_specs, out_specs=out_specs, check_vma=False)
```

```python
import math

import jax
import jax.numpy as jnp
from jax import lax
from jax.experimental import pallas as pl
from jax.experimental.pallas import tpu as pltpu
from jax.sharding import PartitionSpec as P
import functools

C = 256
HI = lax.Precision.HIGHEST


def _factor_block(d, b):
    rows = lax.broadcasted_iota(jnp.int32, (b, 2 * b), 0)
    lanes = lax.broadcasted_iota(jnp.int32, (1, 2 * b), 1)
    x = jnp.concatenate([d, jnp.eye(b, dtype=jnp.float32)], axis=1)
    for j in range(b):
        row = x[j:j + 1, :]
        s = lax.rsqrt(row[:, j:j + 1])
        r = jnp.where(lanes >= j, row * s, 0.0)
        c = jnp.where(rows[:, :1] > j, x[:, j:j + 1] * s, 0.0)
        x = jnp.where(rows == j, r, x - c * r)
    return x[:, :b], x[:, b:]


def _chol_kernel(a_ref, r_ref, w_ref, *, nb, b):
    n = nb * b
    w_ref[...] = a_ref[...]

    def step(k, carry):
        wk = w_ref[k]
        d = jnp.zeros((b, b), jnp.float32)
        for j in range(nb):
            d = jnp.where(k == j, wk[:, j * b:(j + 1) * b], d)
        rkk, linv = _factor_block(d, b)
        pfull = jnp.dot(linv, wk, precision=HI, preferred_element_type=jnp.float32)
        blocks = []
        pblocks = []
        for j in range(nb):
            pj = pfull[:, j * b:(j + 1) * b]
            blocks.append(jnp.where(j > k, pj, jnp.where(j == k, rkk, 0.0)))
            pblocks.append(jnp.where(j > k, pj, 0.0))
        r_ref[k] = jnp.concatenate(blocks, axis=1)
        p = jnp.concatenate(pblocks, axis=1)
        for i in range(1, nb):
            @pl.when(i > k)
            def _():
                ti = pblocks[i]
                upd = lax.dot_general(ti, p[:, i * b:], (((0,), (0,)), ((), ())), precision=HI,
                                      preferred_element_type=jnp.float32)
                w_ref[i, :, i * b:] = w_ref[i, :, i * b:] - upd
        return carry

    lax.fori_loop(0, nb, step, 0)


def cholesky_upper(a, b=128, interpret=False):
    n = a.shape[0]
    nb = n // b
    a3 = a.reshape(nb, b, n)
    out = pl.pallas_call(
        functools.partial(_chol_kernel, nb=nb, b=b),
        out_shape=jax.ShapeDtypeStruct((nb, b, n), jnp.float32),
        in_specs=[pl.BlockSpec(memory_space=pltpu.VMEM)],
        out_specs=pl.BlockSpec(memory_space=pltpu.VMEM),
        scratch_shapes=[pltpu.VMEM((nb, b, n), jnp.float32)],
        compiler_params=pltpu.CompilerParams(vmem_limit_bytes=48 * 1024 * 1024),
        interpret=interpret,
    )(a3)
    return out.reshape(n, n)


def project(images, out_grads, in_signs, out_signs):
    samples, channels, cells = images.shape
    side_in = math.isqrt(cells)
    picture = images.reshape(samples, channels, side_in, side_in)
    width_in = in_signs.shape[1] // 9
    in_matrix = (2 * in_signs - 1).astype(jnp.bfloat16).reshape(channels, 3, 3, width_in)
    kernel = jnp.transpose(in_matrix, (3, 0, 1, 2))
    in_part = lax.conv_general_dilated(
        picture,
        kernel,
        window_strides=(2, 2),
        padding=((1, 1), (1, 1)),
        dimension_numbers=("NCHW", "OIHW", "NCHW"),
        preferred_element_type=jnp.float32,
    )
    in_part = in_part.reshape(samples, width_in, -1)
    out_matrix = (2 * out_signs - 1).astype(jnp.bfloat16)
    out_part = jnp.einsum("ncp,cl->nlp", out_grads, out_matrix, preferred_element_type=jnp.float32)
    return (in_part, out_part)


def sketch(in_sum, out_sum, total_channels):
    in_feat = in_sum / math.sqrt(9 * total_channels)
    out_feat = out_sum / math.sqrt(total_channels)
    cells = in_sum.shape[2]
    outer = jnp.einsum(
        "nlp,njp->nlj", out_feat, in_feat, precision=lax.Precision.HIGHEST
    ) / math.sqrt(cells)
    return outer.reshape(outer.shape[0], -1)


def _ring_order(n):
    if n % 2:
        return list(range(n))
    return list(range(0, n, 2)) + list(range(n - 1, 0, -2))


def ring_reduce_scatter(x, axis, pair):
    n = lax.axis_size(axis)
    order = _ring_order(n)
    me = lax.axis_index(pair)
    pos = jnp.asarray([order.index(c) for c in range(n)], jnp.int32)[lax.axis_index(axis)]
    owner = jnp.asarray(order, jnp.int32)
    blocks = x.reshape(n, -1, x.shape[-1])
    ring = []
    for q in range(n):
        ring.append((order[q] * 2, order[(q + 1) % n] * 2))
        ring.append((order[(q + 1) % n] * 2 + 1, order[q] * 2 + 1))
    sign = 1 - 2 * me

    def take(step):
        q = (pos - sign * (1 + step) + 2 * n) % n
        return lax.dynamic_index_in_dim(blocks, owner[q], 0, keepdims=False)

    acc = take(0)
    for step in range(1, n):
        acc = lax.ppermute(acc, (axis, pair), ring) + take(step)
    return acc


def doubling_gather(x, axes):
    size = 1
    for a in axes:
        size *= lax.axis_size(a)
    if size & (size - 1):
        return lax.all_gather(x, axes, axis=0, tiled=True)
    k = size // 2
    while k:
        other = lax.ppermute(x, axes, [(i, i ^ k) for i in range(size)])
        x = jnp.concatenate([x, other], axis=0)
        k //= 2
    return x


def local(images, out_grads, in_signs, out_signs):
    samples = images.shape[0]
    in_part, out_part = project(images, out_grads, in_signs, out_signs)
    width_in = in_part.shape[1]
    both = jnp.concatenate([in_part, out_part], axis=1).reshape(samples, -1)
    both = ring_reduce_scatter(both, "chan", "samp")
    both = both.reshape(both.shape[0], -1, in_part.shape[2])
    in_sum = both[:, :width_in]
    out_sum = both[:, width_in:]
    own = sketch(in_sum, out_sum, C)
    every = doubling_gather(own, ("chan", "samp"))
    batch_total = samples * lax.axis_size("samp")
    width = every.shape[1]
    identity_mat = jnp.eye(width, dtype=jnp.float32)
    gram = jnp.einsum("nk,nm->km", every, every, precision=lax.Precision.HIGHEST) / batch_total
    factor = cholesky_upper(gram + identity_mat)
    chan_count = lax.axis_size("chan")
    rows_here = width // chan_count
    r_rows = lax.dynamic_slice_in_dim(factor, lax.axis_index("chan") * rows_here, rows_here, 0)
    return (own[None], r_rows)


def solution(mesh):
    in_specs = (
        P(("parts", "samp"), "chan", None),
        P(("parts", "samp"), "chan", None),
        P("chan", None),
        P("chan", None),
    )
    out_specs = (P("samp", ("parts", "chan"), None), P(("parts", "chan"), None))
    return jax.shard_map(local, mesh=mesh, in_specs=in_specs, out_specs=out_specs, check_vma=False)
```

```python
import math

import jax
import jax.numpy as jnp
from jax import lax
from jax.experimental import pallas as pl
from jax.experimental.pallas import tpu as pltpu
from jax.sharding import PartitionSpec as P
import functools

C = 256
HI = lax.Precision.HIGHEST


def _factor_block(d, b):
    rows = lax.broadcasted_iota(jnp.int32, (b, 2 * b), 0)
    lanes = lax.broadcasted_iota(jnp.int32, (1, 2 * b), 1)
    x = jnp.concatenate([d, jnp.eye(b, dtype=jnp.float32)], axis=1)
    for j in range(b):
        row = x[j:j + 1, :]
        s = lax.rsqrt(row[:, j:j + 1])
        r = jnp.where(lanes >= j, row * s, 0.0)
        c = jnp.where(rows[:, :1] > j, x[:, j:j + 1] * s, 0.0)
        x = jnp.where(rows == j, r, x - c * r)
    return x[:, :b], x[:, b:]


def _chol_kernel(a_ref, r_ref, w_ref, *, nb, b):
    n = nb * b
    w_ref[...] = a_ref[...]

    def step(k, carry):
        wk = w_ref[k]
        d = jnp.zeros((b, b), jnp.float32)
        for j in range(nb):
            d = jnp.where(k == j, wk[:, j * b:(j + 1) * b], d)
        rkk, linv = _factor_block(d, b)
        pfull = jnp.dot(linv, wk, precision=HI, preferred_element_type=jnp.float32)
        blocks = []
        pblocks = []
        for j in range(nb):
            pj = pfull[:, j * b:(j + 1) * b]
            blocks.append(jnp.where(j > k, pj, jnp.where(j == k, rkk, 0.0)))
            pblocks.append(jnp.where(j > k, pj, 0.0))
        r_ref[k] = jnp.concatenate(blocks, axis=1)
        p = jnp.concatenate(pblocks, axis=1)
        for i in range(1, nb):
            @pl.when(i > k)
            def _():
                ti = pblocks[i]
                upd = lax.dot_general(ti, p[:, i * b:], (((0,), (0,)), ((), ())), precision=HI,
                                      preferred_element_type=jnp.float32)
                w_ref[i, :, i * b:] = w_ref[i, :, i * b:] - upd
        return carry

    lax.fori_loop(0, nb, step, 0)


def cholesky_upper(a, b=128, interpret=False):
    n = a.shape[0]
    nb = n // b
    a3 = a.reshape(nb, b, n)
    out = pl.pallas_call(
        functools.partial(_chol_kernel, nb=nb, b=b),
        out_shape=jax.ShapeDtypeStruct((nb, b, n), jnp.float32),
        in_specs=[pl.BlockSpec(memory_space=pltpu.VMEM)],
        out_specs=pl.BlockSpec(memory_space=pltpu.VMEM),
        scratch_shapes=[pltpu.VMEM((nb, b, n), jnp.float32)],
        compiler_params=pltpu.CompilerParams(vmem_limit_bytes=48 * 1024 * 1024),
        interpret=interpret,
    )(a3)
    return out.reshape(n, n)


def project(images, out_grads, in_signs, out_signs):
    samples, channels, cells = images.shape
    side_in = math.isqrt(cells)
    picture = images.reshape(samples, channels, side_in, side_in)
    width_in = in_signs.shape[1] // 9
    in_matrix = (2 * in_signs - 1).astype(jnp.bfloat16).reshape(channels, 3, 3, width_in)
    kernel = jnp.transpose(in_matrix, (3, 0, 1, 2))
    in_part = lax.conv_general_dilated(
        picture,
        kernel,
        window_strides=(2, 2),
        padding=((1, 1), (1, 1)),
        dimension_numbers=("NCHW", "OIHW", "NCHW"),
        preferred_element_type=jnp.float32,
    )
    in_part = in_part.reshape(samples, width_in, -1)
    out_matrix = (2 * out_signs - 1).astype(jnp.bfloat16)
    out_part = jnp.einsum("ncp,cl->nlp", out_grads, out_matrix, preferred_element_type=jnp.float32)
    return (in_part, out_part)


def sketch(in_sum, out_sum, total_channels):
    in_feat = in_sum / math.sqrt(9 * total_channels)
    out_feat = out_sum / math.sqrt(total_channels)
    cells = in_sum.shape[2]
    outer = jnp.einsum(
        "nlp,njp->nlj", out_feat, in_feat, precision=lax.Precision.HIGHEST
    ) / math.sqrt(cells)
    return outer.reshape(outer.shape[0], -1)


def _ring_order(n):
    if n % 2:
        return list(range(n))
    return list(range(0, n, 2)) + list(range(n - 1, 0, -2))


def ring_reduce_scatter(x, axis, pair):
    n = lax.axis_size(axis)
    order = _ring_order(n)
    me = lax.axis_index(pair)
    pos = jnp.asarray([order.index(c) for c in range(n)], jnp.int32)[lax.axis_index(axis)]
    owner = jnp.asarray(order, jnp.int32)
    blocks = x.reshape(n, -1, x.shape[-1])
    ring = []
    for q in range(n):
        ring.append((order[q] * 2, order[(q + 1) % n] * 2))
        ring.append((order[(q + 1) % n] * 2 + 1, order[q] * 2 + 1))
    sign = 1 - 2 * me

    def take(step):
        q = (pos - sign * (1 + step) + 2 * n) % n
        return lax.dynamic_index_in_dim(blocks, owner[q], 0, keepdims=False)

    acc = take(0)
    for step in range(1, n):
        acc = lax.ppermute(acc, (axis, pair), ring) + take(step)
    return acc


def doubling_gather(x, axes):
    size = 1
    for a in axes:
        size *= lax.axis_size(a)
    if size & (size - 1):
        return lax.all_gather(x, axes, axis=0, tiled=True)
    k = size // 2
    while k:
        other = lax.ppermute(x, axes, [(i, i ^ k) for i in range(size)])
        x = jnp.concatenate([x, other], axis=0)
        k //= 2
    return x


def local(images, out_grads, in_signs, out_signs):
    samples = images.shape[0]
    in_part, out_part = project(images, out_grads, in_signs, out_signs)
    width_in = in_part.shape[1]
    cells = in_part.shape[2]
    both = jnp.concatenate([jnp.transpose(in_part, (2, 1, 0)), jnp.transpose(out_part, (2, 1, 0))], axis=1)
    both = both.reshape(-1, samples).T
    both = ring_reduce_scatter(both, "chan", "samp")
    both = jnp.transpose(both.reshape(both.shape[0], cells, -1), (0, 2, 1))
    in_sum = both[:, :width_in]
    out_sum = both[:, width_in:]
    own = sketch(in_sum, out_sum, C)
    every = doubling_gather(own, ("chan", "samp"))
    batch_total = samples * lax.axis_size("samp")
    width = every.shape[1]
    identity_mat = jnp.eye(width, dtype=jnp.float32)
    gram = jnp.einsum("nk,nm->km", every, every, precision=lax.Precision.HIGHEST) / batch_total
    factor = cholesky_upper(gram + identity_mat)
    chan_count = lax.axis_size("chan")
    rows_here = width // chan_count
    r_rows = lax.dynamic_slice_in_dim(factor, lax.axis_index("chan") * rows_here, rows_here, 0)
    return (own[None], r_rows)


def solution(mesh):
    in_specs = (
        P(("parts", "samp"), "chan", None),
        P(("parts", "samp"), "chan", None),
        P("chan", None),
        P("chan", None),
    )
    out_specs = (P("samp", ("parts", "chan"), None), P(("parts", "chan"), None))
    return jax.shard_map(local, mesh=mesh, in_specs=in_specs, out_specs=out_specs, check_vma=False)
```

```python
import math

import jax
import jax.numpy as jnp
from jax import lax
from jax.experimental import pallas as pl
from jax.experimental.pallas import tpu as pltpu
from jax.sharding import PartitionSpec as P
import functools

C = 256
HI = lax.Precision.HIGHEST


def _factor_block(d, b):
    rows = lax.broadcasted_iota(jnp.int32, (b, 2 * b), 0)
    lanes = lax.broadcasted_iota(jnp.int32, (1, 2 * b), 1)
    x = jnp.concatenate([d, jnp.eye(b, dtype=jnp.float32)], axis=1)
    for j in range(b):
        row = x[j:j + 1, :]
        s = lax.rsqrt(row[:, j:j + 1])
        r = jnp.where(lanes >= j, row * s, 0.0)
        c = jnp.where(rows[:, :1] > j, x[:, j:j + 1] * s, 0.0)
        x = jnp.where(rows == j, r, x - c * r)
    return x[:, :b], x[:, b:]


def _chol_kernel(a_ref, r_ref, w_ref, *, nb, b):
    w_ref[...] = a_ref[...]

    def panel(k, rkk, linv):
        pfull = rkk
        if k + 1 < nb:
            rest = jnp.dot(linv, w_ref[k][:, (k + 1) * b:], precision=HI,
                           preferred_element_type=jnp.float32)
            pfull = jnp.concatenate([rkk, rest], axis=1)
        r_ref[k] = jnp.concatenate([jnp.zeros((b, k * b), jnp.float32), pfull], axis=1) if k else pfull
        return pfull

    def update(k, p, i):
        ti = p[:, (i - k) * b:(i - k + 1) * b]
        upd = lax.dot_general(ti, p[:, (i - k) * b:], (((0,), (0,)), ((), ())), precision=HI,
                              preferred_element_type=jnp.float32)
        w_ref[i, :, i * b:] = w_ref[i, :, i * b:] - upd

    rkk, linv = _factor_block(w_ref[0][:, :b], b)
    for k in range(nb):
        p = panel(k, rkk, linv)
        if k + 1 < nb:
            update(k, p, k + 1)
            rkk, linv = _factor_block(w_ref[k + 1][:, (k + 1) * b:(k + 2) * b], b)
            for i in range(k + 2, nb):
                update(k, p, i)


def cholesky_upper(a, b=128, interpret=False):
    n = a.shape[0]
    nb = n // b
    a3 = a.reshape(nb, b, n)
    out = pl.pallas_call(
        functools.partial(_chol_kernel, nb=nb, b=b),
        out_shape=jax.ShapeDtypeStruct((nb, b, n), jnp.float32),
        in_specs=[pl.BlockSpec(memory_space=pltpu.VMEM)],
        out_specs=pl.BlockSpec(memory_space=pltpu.VMEM),
        scratch_shapes=[pltpu.VMEM((nb, b, n), jnp.float32)],
        compiler_params=pltpu.CompilerParams(vmem_limit_bytes=48 * 1024 * 1024),
        interpret=interpret,
    )(a3)
    return out.reshape(n, n)


def project(images, out_grads, in_signs, out_signs):
    samples, channels, cells = images.shape
    side_in = math.isqrt(cells)
    picture = images.reshape(samples, channels, side_in, side_in)
    width_in = in_signs.shape[1] // 9
    in_matrix = (2 * in_signs - 1).astype(jnp.bfloat16).reshape(channels, 3, 3, width_in)
    kernel = jnp.transpose(in_matrix, (3, 0, 1, 2))
    in_part = lax.conv_general_dilated(
        picture,
        kernel,
        window_strides=(2, 2),
        padding=((1, 1), (1, 1)),
        dimension_numbers=("NCHW", "OIHW", "NCHW"),
        preferred_element_type=jnp.float32,
    )
    in_part = in_part.reshape(samples, width_in, -1)
    out_matrix = (2 * out_signs - 1).astype(jnp.bfloat16)
    out_part = jnp.einsum("ncp,cl->nlp", out_grads, out_matrix, preferred_element_type=jnp.float32)
    return (in_part, out_part)


def sketch(in_sum, out_sum, total_channels):
    in_feat = in_sum / math.sqrt(9 * total_channels)
    out_feat = out_sum / math.sqrt(total_channels)
    cells = in_sum.shape[2]
    outer = jnp.einsum(
        "nlp,njp->nlj", out_feat, in_feat, precision=lax.Precision.HIGHEST
    ) / math.sqrt(cells)
    return outer.reshape(outer.shape[0], -1)


def _ring_order(n):
    if n % 2:
        return list(range(n))
    return list(range(0, n, 2)) + list(range(n - 1, 0, -2))


def ring_reduce_scatter(x, axis, pair):
    n = lax.axis_size(axis)
    order = _ring_order(n)
    me = lax.axis_index(pair)
    pos = jnp.asarray([order.index(c) for c in range(n)], jnp.int32)[lax.axis_index(axis)]
    owner = jnp.asarray(order, jnp.int32)
    blocks = x.reshape(n, -1, x.shape[-1])
    ring = []
    for q in range(n):
        ring.append((order[q] * 2, order[(q + 1) % n] * 2))
        ring.append((order[(q + 1) % n] * 2 + 1, order[q] * 2 + 1))
    sign = 1 - 2 * me

    def take(step):
        q = (pos - sign * (1 + step) + 2 * n) % n
        return lax.dynamic_index_in_dim(blocks, owner[q], 0, keepdims=False)

    acc = take(0)
    for step in range(1, n):
        acc = lax.ppermute(acc, (axis, pair), ring) + take(step)
    return acc


def doubling_gather(x, axes):
    size = 1
    for a in axes:
        size *= lax.axis_size(a)
    if size & (size - 1):
        return lax.all_gather(x, axes, axis=0, tiled=True)
    k = size // 2
    while k:
        other = lax.ppermute(x, axes, [(i, i ^ k) for i in range(size)])
        x = jnp.concatenate([x, other], axis=0)
        k //= 2
    return x


def local(images, out_grads, in_signs, out_signs):
    samples = images.shape[0]
    in_part, out_part = project(images, out_grads, in_signs, out_signs)
    width_in = in_part.shape[1]
    cells = in_part.shape[2]
    both = jnp.concatenate([jnp.transpose(in_part, (2, 1, 0)), jnp.transpose(out_part, (2, 1, 0))], axis=1)
    both = both.reshape(-1, samples).T
    both = ring_reduce_scatter(both, "chan", "samp")
    both = jnp.transpose(both.reshape(both.shape[0], cells, -1), (0, 2, 1))
    in_sum = both[:, :width_in]
    out_sum = both[:, width_in:]
    own = sketch(in_sum, out_sum, C)
    every = doubling_gather(own, ("chan", "samp"))
    batch_total = samples * lax.axis_size("samp")
    width = every.shape[1]
    identity_mat = jnp.eye(width, dtype=jnp.float32)
    gram = jnp.einsum("nk,nm->km", every, every, precision=lax.Precision.HIGHEST) / batch_total
    factor = cholesky_upper(gram + identity_mat)
    chan_count = lax.axis_size("chan")
    rows_here = width // chan_count
    r_rows = lax.dynamic_slice_in_dim(factor, lax.axis_index("chan") * rows_here, rows_here, 0)
    return (own[None], r_rows)


def solution(mesh):
    in_specs = (
        P(("parts", "samp"), "chan", None),
        P(("parts", "samp"), "chan", None),
        P("chan", None),
        P("chan", None),
    )
    out_specs = (P("samp", ("parts", "chan"), None), P(("parts", "chan"), None))
    return jax.shard_map(local, mesh=mesh, in_specs=in_specs, out_specs=out_specs, check_vma=False)
```

```python
import math

import jax
import jax.numpy as jnp
from jax import lax
from jax.experimental import pallas as pl
from jax.experimental.pallas import tpu as pltpu
from jax.sharding import PartitionSpec as P
import functools

C = 256
HI = lax.Precision.HIGHEST


def _factor_block(d, b):
    rows = lax.broadcasted_iota(jnp.int32, (b, 2 * b), 0)
    lanes = lax.broadcasted_iota(jnp.int32, (1, 2 * b), 1)
    x = jnp.concatenate([d, jnp.eye(b, dtype=jnp.float32)], axis=1)
    for j in range(b):
        row = x[j:j + 1, :]
        s = lax.rsqrt(row[:, j:j + 1])
        r = jnp.where(lanes >= j, row * s, 0.0)
        c = jnp.where(rows[:, :1] > j, x[:, j:j + 1] * s, 0.0)
        x = jnp.where(rows == j, r, x - c * r)
    return x[:, :b], x[:, b:]


def _chol_kernel(f_ref, r_ref, w_ref, *, nb, b, scale):
    n = nb * b
    f = f_ref[...]
    eye = jnp.eye(b, dtype=jnp.float32)
    for i in range(nb):
        g = lax.dot_general(f[:, i * b:(i + 1) * b], f, (((0,), (0,)), ((), ())), precision=HI,
                            preferred_element_type=jnp.float32) * scale
        w_ref[i] = g
        w_ref[i, :, i * b:(i + 1) * b] = g[:, i * b:(i + 1) * b] + eye

    def step(k, carry):
        wk = w_ref[k]
        d = jnp.zeros((b, b), jnp.float32)
        for j in range(nb):
            d = jnp.where(k == j, wk[:, j * b:(j + 1) * b], d)
        rkk, linv = _factor_block(d, b)
        pfull = jnp.dot(linv, wk, precision=HI, preferred_element_type=jnp.float32)
        blocks = []
        pblocks = []
        for j in range(nb):
            pj = pfull[:, j * b:(j + 1) * b]
            blocks.append(jnp.where(j > k, pj, jnp.where(j == k, rkk, 0.0)))
            pblocks.append(jnp.where(j > k, pj, 0.0))
        r_ref[k] = jnp.concatenate(blocks, axis=1)
        p = jnp.concatenate(pblocks, axis=1)
        for i in range(1, nb):
            @pl.when(i > k)
            def _():
                ti = pblocks[i]
                upd = lax.dot_general(ti, p[:, i * b:], (((0,), (0,)), ((), ())), precision=HI,
                                      preferred_element_type=jnp.float32)
                w_ref[i, :, i * b:] = w_ref[i, :, i * b:] - upd
        return carry

    lax.fori_loop(0, nb, step, 0)


def damped_cholesky(f, scale, b=128, interpret=False):
    n = f.shape[1]
    nb = n // b
    out = pl.pallas_call(
        functools.partial(_chol_kernel, nb=nb, b=b, scale=scale),
        out_shape=jax.ShapeDtypeStruct((nb, b, n), jnp.float32),
        in_specs=[pl.BlockSpec(memory_space=pltpu.VMEM)],
        out_specs=pl.BlockSpec(memory_space=pltpu.VMEM),
        scratch_shapes=[pltpu.VMEM((nb, b, n), jnp.float32)],
        compiler_params=pltpu.CompilerParams(vmem_limit_bytes=48 * 1024 * 1024),
        interpret=interpret,
    )(f)
    return out.reshape(n, n)


def project(images, out_grads, in_signs, out_signs):
    samples, channels, cells = images.shape
    side_in = math.isqrt(cells)
    picture = images.reshape(samples, channels, side_in, side_in)
    width_in = in_signs.shape[1] // 9
    in_matrix = (2 * in_signs - 1).astype(jnp.bfloat16).reshape(channels, 3, 3, width_in)
    kernel = jnp.transpose(in_matrix, (3, 0, 1, 2))
    in_part = lax.conv_general_dilated(
        picture,
        kernel,
        window_strides=(2, 2),
        padding=((1, 1), (1, 1)),
        dimension_numbers=("NCHW", "OIHW", "NCHW"),
        preferred_element_type=jnp.float32,
    )
    in_part = in_part.reshape(samples, width_in, -1)
    out_matrix = (2 * out_signs - 1).astype(jnp.bfloat16)
    out_part = jnp.einsum("ncp,cl->nlp", out_grads, out_matrix, preferred_element_type=jnp.float32)
    return (in_part, out_part)


def sketch(in_sum, out_sum, total_channels):
    in_feat = in_sum / math.sqrt(9 * total_channels)
    out_feat = out_sum / math.sqrt(total_channels)
    cells = in_sum.shape[2]
    outer = jnp.einsum(
        "nlp,njp->nlj", out_feat, in_feat, precision=lax.Precision.HIGHEST
    ) / math.sqrt(cells)
    return outer.reshape(outer.shape[0], -1)


def _ring_order(n):
    if n % 2:
        return list(range(n))
    return list(range(0, n, 2)) + list(range(n - 1, 0, -2))


def ring_reduce_scatter(x, axis, pair):
    n = lax.axis_size(axis)
    order = _ring_order(n)
    me = lax.axis_index(pair)
    pos = jnp.asarray([order.index(c) for c in range(n)], jnp.int32)[lax.axis_index(axis)]
    owner = jnp.asarray(order, jnp.int32)
    blocks = x.reshape(n, -1, x.shape[-1])
    ring = []
    for q in range(n):
        ring.append((order[q] * 2, order[(q + 1) % n] * 2))
        ring.append((order[(q + 1) % n] * 2 + 1, order[q] * 2 + 1))
    sign = 1 - 2 * me

    def take(step):
        q = (pos - sign * (1 + step) + 2 * n) % n
        return lax.dynamic_index_in_dim(blocks, owner[q], 0, keepdims=False)

    acc = take(0)
    for step in range(1, n):
        acc = lax.ppermute(acc, (axis, pair), ring) + take(step)
    return acc


def doubling_gather(x, axes):
    size = 1
    for a in axes:
        size *= lax.axis_size(a)
    if size & (size - 1):
        return lax.all_gather(x, axes, axis=0, tiled=True)
    k = size // 2
    while k:
        other = lax.ppermute(x, axes, [(i, i ^ k) for i in range(size)])
        x = jnp.concatenate([x, other], axis=0)
        k //= 2
    return x


def local(images, out_grads, in_signs, out_signs):
    samples = images.shape[0]
    in_part, out_part = project(images, out_grads, in_signs, out_signs)
    width_in = in_part.shape[1]
    cells = in_part.shape[2]
    both = jnp.concatenate([jnp.transpose(in_part, (2, 1, 0)), jnp.transpose(out_part, (2, 1, 0))], axis=1)
    both = both.reshape(-1, samples).T
    both = ring_reduce_scatter(both, "chan", "samp")
    both = jnp.transpose(both.reshape(both.shape[0], cells, -1), (0, 2, 1))
    in_sum = both[:, :width_in]
    out_sum = both[:, width_in:]
    own = sketch(in_sum, out_sum, C)
    every = doubling_gather(own, ("chan", "samp"))
    batch_total = samples * lax.axis_size("samp")
    width = every.shape[1]
    factor = damped_cholesky(every, 1.0 / batch_total)
    chan_count = lax.axis_size("chan")
    rows_here = width // chan_count
    r_rows = lax.dynamic_slice_in_dim(factor, lax.axis_index("chan") * rows_here, rows_here, 0)
    return (own[None], r_rows)


def solution(mesh):
    in_specs = (
        P(("parts", "samp"), "chan", None),
        P(("parts", "samp"), "chan", None),
        P("chan", None),
        P("chan", None),
    )
    out_specs = (P("samp", ("parts", "chan"), None), P(("parts", "chan"), None))
    return jax.shard_map(local, mesh=mesh, in_specs=in_specs, out_specs=out_specs, check_vma=False)
```

```python
import math

import jax
import jax.numpy as jnp
from jax import lax
from jax.experimental import pallas as pl
from jax.experimental.pallas import tpu as pltpu
from jax.sharding import PartitionSpec as P
import functools

C = 256
HI = lax.Precision.HIGHEST


def _factor_block(d, b):
    rows = lax.broadcasted_iota(jnp.int32, (b, 2 * b), 0)
    lanes = lax.broadcasted_iota(jnp.int32, (1, 2 * b), 1)
    x = jnp.concatenate([d, jnp.eye(b, dtype=jnp.float32)], axis=1)
    for j in range(b):
        row = x[j:j + 1, :]
        s = lax.rsqrt(row[:, j:j + 1])
        r = jnp.where(lanes >= j, row * s, 0.0)
        c = jnp.where(rows[:, :1] > j, x[:, j:j + 1] * s, 0.0)
        x = jnp.where(rows == j, r, x - c * r)
    return x[:, :b], x[:, b:]


def _chol_kernel(f_ref, c_ref, o_ref, w_ref, r_ref, *, nb, b, scale):
    n = nb * b
    f = f_ref[...]
    eye = jnp.eye(b, dtype=jnp.float32)
    for i in range(nb):
        g = lax.dot_general(f[:, i * b:(i + 1) * b], f, (((0,), (0,)), ((), ())), precision=HI,
                            preferred_element_type=jnp.float32) * scale
        w_ref[i] = g
        w_ref[i, :, i * b:(i + 1) * b] = g[:, i * b:(i + 1) * b] + eye

    def step(k, carry):
        wk = w_ref[k]
        d = jnp.zeros((b, b), jnp.float32)
        for j in range(nb):
            d = jnp.where(k == j, wk[:, j * b:(j + 1) * b], d)
        rkk, linv = _factor_block(d, b)
        pfull = jnp.dot(linv, wk, precision=HI, preferred_element_type=jnp.float32)
        blocks = []
        pblocks = []
        for j in range(nb):
            pj = pfull[:, j * b:(j + 1) * b]
            blocks.append(jnp.where(j > k, pj, jnp.where(j == k, rkk, 0.0)))
            pblocks.append(jnp.where(j > k, pj, 0.0))
        r_ref[pl.ds(pl.multiple_of(k * b, b), b), :] = jnp.concatenate(blocks, axis=1)
        p = jnp.concatenate(pblocks, axis=1)
        for i in range(1, nb):
            @pl.when(i > k)
            def _():
                ti = pblocks[i]
                upd = lax.dot_general(ti, p[:, i * b:], (((0,), (0,)), ((), ())), precision=HI,
                                      preferred_element_type=jnp.float32)
                w_ref[i, :, i * b:] = w_ref[i, :, i * b:] - upd
        return carry

    lax.fori_loop(0, nb, step, 0)
    rows = o_ref.shape[0]
    o_ref[...] = r_ref[pl.ds(pl.multiple_of(c_ref[0] * rows, 8), rows), :]


def damped_cholesky(f, scale, part, parts, b=128, interpret=False):
    n = f.shape[1]
    nb = n // b
    rows = n // parts
    return pl.pallas_call(
        functools.partial(_chol_kernel, nb=nb, b=b, scale=scale),
        out_shape=jax.ShapeDtypeStruct((rows, n), jnp.float32),
        in_specs=[pl.BlockSpec(memory_space=pltpu.VMEM), pl.BlockSpec(memory_space=pltpu.SMEM)],
        out_specs=pl.BlockSpec(memory_space=pltpu.VMEM),
        scratch_shapes=[pltpu.VMEM((nb, b, n), jnp.float32), pltpu.VMEM((n, n), jnp.float32)],
        compiler_params=pltpu.CompilerParams(vmem_limit_bytes=48 * 1024 * 1024),
        interpret=interpret,
    )(f, jnp.reshape(part, (1,)).astype(jnp.int32))


def project(images, out_grads, in_signs, out_signs):
    samples, channels, cells = images.shape
    side_in = math.isqrt(cells)
    picture = images.reshape(samples, channels, side_in, side_in)
    width_in = in_signs.shape[1] // 9
    in_matrix = (2 * in_signs - 1).astype(jnp.bfloat16).reshape(channels, 3, 3, width_in)
    kernel = jnp.transpose(in_matrix, (3, 0, 1, 2))
    in_part = lax.conv_general_dilated(
        picture,
        kernel,
        window_strides=(2, 2),
        padding=((1, 1), (1, 1)),
        dimension_numbers=("NCHW", "OIHW", "NCHW"),
        preferred_element_type=jnp.float32,
    )
    in_part = in_part.reshape(samples, width_in, -1)
    out_matrix = (2 * out_signs - 1).astype(jnp.bfloat16)
    out_part = jnp.einsum("ncp,cl->nlp", out_grads, out_matrix, preferred_element_type=jnp.float32)
    return (in_part, out_part)


def sketch(in_sum, out_sum, total_channels):
    in_feat = in_sum / math.sqrt(9 * total_channels)
    out_feat = out_sum / math.sqrt(total_channels)
    cells = in_sum.shape[2]
    outer = jnp.einsum(
        "nlp,njp->nlj", out_feat, in_feat, precision=lax.Precision.HIGHEST
    ) / math.sqrt(cells)
    return outer.reshape(outer.shape[0], -1)


def _ring_order(n):
    if n % 2:
        return list(range(n))
    return list(range(0, n, 2)) + list(range(n - 1, 0, -2))


def ring_reduce_scatter(x, axis, pair):
    n = lax.axis_size(axis)
    order = _ring_order(n)
    me = lax.axis_index(pair)
    pos = jnp.asarray([order.index(c) for c in range(n)], jnp.int32)[lax.axis_index(axis)]
    owner = jnp.asarray(order, jnp.int32)
    blocks = x.reshape(n, -1, x.shape[-1])
    ring = []
    for q in range(n):
        ring.append((order[q] * 2, order[(q + 1) % n] * 2))
        ring.append((order[(q + 1) % n] * 2 + 1, order[q] * 2 + 1))
    sign = 1 - 2 * me

    def take(step):
        q = (pos - sign * (1 + step) + 2 * n) % n
        return lax.dynamic_index_in_dim(blocks, owner[q], 0, keepdims=False)

    acc = take(0)
    for step in range(1, n):
        acc = lax.ppermute(acc, (axis, pair), ring) + take(step)
    return acc


def doubling_gather(x, axes):
    size = 1
    for a in axes:
        size *= lax.axis_size(a)
    if size & (size - 1):
        return lax.all_gather(x, axes, axis=0, tiled=True)
    k = size // 2
    while k:
        other = lax.ppermute(x, axes, [(i, i ^ k) for i in range(size)])
        x = jnp.concatenate([x, other], axis=0)
        k //= 2
    return x


def local(images, out_grads, in_signs, out_signs):
    samples = images.shape[0]
    in_part, out_part = project(images, out_grads, in_signs, out_signs)
    width_in = in_part.shape[1]
    cells = in_part.shape[2]
    both = jnp.concatenate([jnp.transpose(in_part, (2, 1, 0)), jnp.transpose(out_part, (2, 1, 0))], axis=1)
    both = both.reshape(-1, samples).T
    both = ring_reduce_scatter(both, "chan", "samp")
    both = jnp.transpose(both.reshape(both.shape[0], cells, -1), (0, 2, 1))
    in_sum = both[:, :width_in]
    out_sum = both[:, width_in:]
    own = sketch(in_sum, out_sum, C)
    every = doubling_gather(own, ("chan", "samp"))
    batch_total = samples * lax.axis_size("samp")
    width = every.shape[1]
    r_rows = damped_cholesky(every, 1.0 / batch_total, lax.axis_index("chan"), lax.axis_size("chan"))
    return (own[None], r_rows)


def solution(mesh):
    in_specs = (
        P(("parts", "samp"), "chan", None),
        P(("parts", "samp"), "chan", None),
        P("chan", None),
        P("chan", None),
    )
    out_specs = (P("samp", ("parts", "chan"), None), P(("parts", "chan"), None))
    return jax.shard_map(local, mesh=mesh, in_specs=in_specs, out_specs=out_specs, check_vma=False)
```

```python
import math

import jax
import jax.numpy as jnp
from jax import lax
from jax.experimental import pallas as pl
from jax.experimental.pallas import tpu as pltpu
from jax.sharding import PartitionSpec as P
import functools

C = 256
HI = lax.Precision.HIGHEST


def _factor_block(d, b):
    rows = lax.broadcasted_iota(jnp.int32, (b, 2 * b), 0)
    lanes = lax.broadcasted_iota(jnp.int32, (1, 2 * b), 1)
    x = jnp.concatenate([d, jnp.eye(b, dtype=jnp.float32)], axis=1)
    for j in range(b):
        row = x[j:j + 1, :]
        s = lax.rsqrt(row[:, j:j + 1])
        r = jnp.where(lanes >= j, row * s, 0.0)
        c = jnp.where(rows[:, :1] > j, x[:, j:j + 1] * s, 0.0)
        x = jnp.where(rows == j, r, x - c * r)
    return x[:, :b], x[:, b:]


def _chol_kernel(f_ref, c_ref, o_ref, w_ref, r_ref, *, nb, b, scale):
    n = nb * b
    f = f_ref[...]
    eye = jnp.eye(b, dtype=jnp.float32)
    for i in range(nb):
        g = lax.dot_general(f[:, i * b:(i + 1) * b], f, (((0,), (0,)), ((), ())), precision=HI,
                            preferred_element_type=jnp.float32) * scale
        w_ref[i] = g
        w_ref[i, :, i * b:(i + 1) * b] = g[:, i * b:(i + 1) * b] + eye

    def step(k, carry):
        wk = w_ref[k]
        d = jnp.zeros((b, b), jnp.float32)
        for j in range(nb):
            d = jnp.where(k == j, wk[:, j * b:(j + 1) * b], d)
        rkk, linv = _factor_block(d, b)
        pfull = jnp.dot(linv, wk, precision=HI, preferred_element_type=jnp.float32)
        blocks = []
        pblocks = []
        for j in range(nb):
            pj = pfull[:, j * b:(j + 1) * b]
            blocks.append(jnp.where(j > k, pj, jnp.where(j == k, rkk, 0.0)))
            pblocks.append(jnp.where(j > k, pj, 0.0))
        r_ref[pl.ds(pl.multiple_of(k * b, b), b), :] = jnp.concatenate(blocks, axis=1)
        p = jnp.concatenate(pblocks, axis=1)
        for i in range(1, nb):
            @pl.when(i > k)
            def _():
                ti = pblocks[i]
                upd = lax.dot_general(ti, p[:, i * b:], (((0,), (0,)), ((), ())), precision=HI,
                                      preferred_element_type=jnp.float32)
                w_ref[i, :, i * b:] = w_ref[i, :, i * b:] - upd
        return carry

    lax.fori_loop(0, nb, step, 0)
    rows = o_ref.shape[0]
    o_ref[...] = r_ref[pl.ds(pl.multiple_of(c_ref[0] * rows, 8), rows), :]


def damped_cholesky(f, scale, part, parts, b=128, interpret=False):
    n = f.shape[1]
    nb = n // b
    rows = n // parts
    return pl.pallas_call(
        functools.partial(_chol_kernel, nb=nb, b=b, scale=scale),
        out_shape=jax.ShapeDtypeStruct((rows, n), jnp.float32),
        in_specs=[pl.BlockSpec(memory_space=pltpu.VMEM), pl.BlockSpec(memory_space=pltpu.SMEM)],
        out_specs=pl.BlockSpec(memory_space=pltpu.VMEM),
        scratch_shapes=[pltpu.VMEM((nb, b, n), jnp.float32), pltpu.VMEM((n, n), jnp.float32)],
        compiler_params=pltpu.CompilerParams(vmem_limit_bytes=48 * 1024 * 1024),
        interpret=interpret,
    )(f, jnp.reshape(part, (1,)).astype(jnp.int32))


def project(images, out_grads, in_signs, out_signs):
    samples, channels, cells = images.shape
    side_in = math.isqrt(cells)
    picture = images.reshape(samples, channels, side_in, side_in)
    width_in = in_signs.shape[1] // 9
    in_matrix = (2 * in_signs - 1).astype(jnp.bfloat16).reshape(channels, 3, 3, width_in)
    kernel = jnp.transpose(in_matrix, (3, 0, 1, 2))
    in_part = lax.conv_general_dilated(
        picture,
        kernel,
        window_strides=(2, 2),
        padding=((1, 1), (1, 1)),
        dimension_numbers=("NCHW", "OIHW", "NCHW"),
        preferred_element_type=jnp.float32,
    )
    in_part = in_part.reshape(samples, width_in, -1)
    out_matrix = (2 * out_signs - 1).astype(jnp.bfloat16)
    out_part = jnp.einsum("ncp,cl->nlp", out_grads, out_matrix, preferred_element_type=jnp.float32)
    return (in_part, out_part)


def sketch(in_sum, out_sum, total_channels):
    in_feat = in_sum / math.sqrt(9 * total_channels)
    out_feat = out_sum / math.sqrt(total_channels)
    cells = in_sum.shape[2]
    outer = jnp.einsum(
        "nlp,njp->nlj", out_feat, in_feat, precision=lax.Precision.HIGHEST
    ) / math.sqrt(cells)
    return outer.reshape(outer.shape[0], -1)


def _ring_order(n):
    if n % 2:
        return list(range(n))
    return list(range(0, n, 2)) + list(range(n - 1, 0, -2))


def ring_reduce_scatter(xt, axis, pair):
    n = lax.axis_size(axis)
    order = _ring_order(n)
    me = lax.axis_index(pair)
    pos = jnp.asarray([order.index(c) for c in range(n)], jnp.int32)[lax.axis_index(axis)]
    owner = jnp.asarray(order, jnp.int32)
    m = xt.shape[1] // n
    ring = []
    for q in range(n):
        ring.append((order[q] * 2, order[(q + 1) % n] * 2))
        ring.append((order[(q + 1) % n] * 2 + 1, order[q] * 2 + 1))
    sign = 1 - 2 * me

    def take(step):
        q = (pos - sign * (1 + step) + 2 * n) % n
        return lax.dynamic_slice_in_dim(xt, owner[q] * m, m, axis=1).T

    acc = take(0)
    for step in range(1, n):
        acc = lax.ppermute(acc, (axis, pair), ring) + take(step)
    return acc


def doubling_gather(x, axes):
    size = 1
    for a in axes:
        size *= lax.axis_size(a)
    if size & (size - 1):
        return lax.all_gather(x, axes, axis=0, tiled=True)
    k = size // 2
    while k:
        other = lax.ppermute(x, axes, [(i, i ^ k) for i in range(size)])
        x = jnp.concatenate([x, other], axis=0)
        k //= 2
    return x


def local(images, out_grads, in_signs, out_signs):
    samples = images.shape[0]
    in_part, out_part = project(images, out_grads, in_signs, out_signs)
    width_in = in_part.shape[1]
    cells = in_part.shape[2]
    both = jnp.concatenate([jnp.transpose(in_part, (2, 1, 0)), jnp.transpose(out_part, (2, 1, 0))], axis=1)
    both = both.reshape(-1, samples)
    both = ring_reduce_scatter(both, "chan", "samp")
    both = jnp.transpose(both.reshape(both.shape[0], cells, -1), (0, 2, 1))
    in_sum = both[:, :width_in]
    out_sum = both[:, width_in:]
    own = sketch(in_sum, out_sum, C)
    every = doubling_gather(own, ("chan", "samp"))
    batch_total = samples * lax.axis_size("samp")
    width = every.shape[1]
    r_rows = damped_cholesky(every, 1.0 / batch_total, lax.axis_index("chan"), lax.axis_size("chan"))
    return (own[None], r_rows)


def solution(mesh):
    in_specs = (
        P(("parts", "samp"), "chan", None),
        P(("parts", "samp"), "chan", None),
        P("chan", None),
        P("chan", None),
    )
    out_specs = (P("samp", ("parts", "chan"), None), P(("parts", "chan"), None))
    return jax.shard_map(local, mesh=mesh, in_specs=in_specs, out_specs=out_specs, check_vma=False)
```

```python
import math

import jax
import jax.numpy as jnp
from jax import lax
from jax.experimental import pallas as pl
from jax.experimental.pallas import tpu as pltpu
from jax.sharding import PartitionSpec as P
import functools

C = 256
HI = lax.Precision.HIGHEST


def _factor_block(d, b):
    rows = lax.broadcasted_iota(jnp.int32, (b, 2 * b), 0)
    lanes = lax.broadcasted_iota(jnp.int32, (1, 2 * b), 1)
    x = jnp.concatenate([d, jnp.eye(b, dtype=jnp.float32)], axis=1)
    for j in range(b):
        row = x[j:j + 1, :]
        s = lax.rsqrt(row[:, j:j + 1])
        r = jnp.where(lanes >= j, row * s, 0.0)
        c = jnp.where(rows[:, :1] > j, x[:, j:j + 1] * s, 0.0)
        x = jnp.where(rows == j, r, x - c * r)
    return x[:, :b], x[:, b:]


def _chol_kernel(f_ref, c_ref, o_ref, w_ref, r_ref, *, nb, b, scale):
    n = nb * b
    f = f_ref[...]
    eye = jnp.eye(b, dtype=jnp.float32)
    for i in range(nb):
        g = lax.dot_general(f[:, i * b:(i + 1) * b], f, (((0,), (0,)), ((), ())), precision=HI,
                            preferred_element_type=jnp.float32) * scale
        w_ref[i] = g
        w_ref[i, :, i * b:(i + 1) * b] = g[:, i * b:(i + 1) * b] + eye

    def diag(k):
        wk = w_ref[k]
        d = jnp.zeros((b, b), jnp.float32)
        for j in range(nb):
            d = jnp.where(k == j, wk[:, j * b:(j + 1) * b], d)
        return d

    def panel(k, rkk, linv):
        pfull = jnp.dot(linv, w_ref[k], precision=HI, preferred_element_type=jnp.float32)
        blocks = []
        pblocks = []
        for j in range(nb):
            pj = pfull[:, j * b:(j + 1) * b]
            blocks.append(jnp.where(j > k, pj, jnp.where(j == k, rkk, 0.0)))
            pblocks.append(jnp.where(j > k, pj, 0.0))
        r_ref[pl.ds(pl.multiple_of(k * b, b), b), :] = jnp.concatenate(blocks, axis=1)
        return pblocks

    def step(k, carry):
        rkk, linv = carry
        pblocks = panel(k, rkk, linv)
        p = jnp.concatenate(pblocks, axis=1)
        t1 = jnp.zeros((b, b), jnp.float32)
        for j in range(nb):
            t1 = jnp.where(k + 1 == j, pblocks[j], t1)
        k1 = k + 1
        w_ref[k1] = w_ref[k1] - lax.dot_general(t1, p, (((0,), (0,)), ((), ())), precision=HI,
                                                preferred_element_type=jnp.float32)
        nxt = _factor_block(diag(k1), b)
        for i in range(2, nb):
            ti = jnp.where(i > k1, pblocks[i], 0.0)
            upd = lax.dot_general(ti, p[:, i * b:], (((0,), (0,)), ((), ())), precision=HI,
                                  preferred_element_type=jnp.float32)
            w_ref[i, :, i * b:] = w_ref[i, :, i * b:] - upd
        return nxt

    last = lax.fori_loop(0, nb - 1, step, _factor_block(diag(0), b))
    panel(nb - 1, *last)
    rows = o_ref.shape[0]
    o_ref[...] = r_ref[pl.ds(pl.multiple_of(c_ref[0] * rows, 8), rows), :]


def damped_cholesky(f, scale, part, parts, b=128, interpret=False):
    n = f.shape[1]
    nb = n // b
    rows = n // parts
    return pl.pallas_call(
        functools.partial(_chol_kernel, nb=nb, b=b, scale=scale),
        out_shape=jax.ShapeDtypeStruct((rows, n), jnp.float32),
        in_specs=[pl.BlockSpec(memory_space=pltpu.VMEM), pl.BlockSpec(memory_space=pltpu.SMEM)],
        out_specs=pl.BlockSpec(memory_space=pltpu.VMEM),
        scratch_shapes=[pltpu.VMEM((nb, b, n), jnp.float32), pltpu.VMEM((n, n), jnp.float32)],
        compiler_params=pltpu.CompilerParams(vmem_limit_bytes=48 * 1024 * 1024),
        interpret=interpret,
    )(f, jnp.reshape(part, (1,)).astype(jnp.int32))


def project(images, out_grads, in_signs, out_signs):
    samples, channels, cells = images.shape
    side_in = math.isqrt(cells)
    picture = images.reshape(samples, channels, side_in, side_in)
    width_in = in_signs.shape[1] // 9
    in_matrix = (2 * in_signs - 1).astype(jnp.bfloat16).reshape(channels, 3, 3, width_in)
    kernel = jnp.transpose(in_matrix, (3, 0, 1, 2))
    in_part = lax.conv_general_dilated(
        picture,
        kernel,
        window_strides=(2, 2),
        padding=((1, 1), (1, 1)),
        dimension_numbers=("NCHW", "OIHW", "NCHW"),
        preferred_element_type=jnp.float32,
    )
    in_part = in_part.reshape(samples, width_in, -1)
    out_matrix = (2 * out_signs - 1).astype(jnp.bfloat16)
    out_part = jnp.einsum("ncp,cl->nlp", out_grads, out_matrix, preferred_element_type=jnp.float32)
    return (in_part, out_part)


def sketch(in_sum, out_sum, total_channels):
    in_feat = in_sum / math.sqrt(9 * total_channels)
    out_feat = out_sum / math.sqrt(total_channels)
    cells = in_sum.shape[2]
    outer = jnp.einsum(
        "nlp,njp->nlj", out_feat, in_feat, precision=lax.Precision.HIGHEST
    ) / math.sqrt(cells)
    return outer.reshape(outer.shape[0], -1)


def _ring_order(n):
    if n % 2:
        return list(range(n))
    return list(range(0, n, 2)) + list(range(n - 1, 0, -2))


def ring_reduce_scatter(x, axis, pair):
    n = lax.axis_size(axis)
    order = _ring_order(n)
    me = lax.axis_index(pair)
    pos = jnp.asarray([order.index(c) for c in range(n)], jnp.int32)[lax.axis_index(axis)]
    owner = jnp.asarray(order, jnp.int32)
    blocks = x.reshape(n, -1, x.shape[-1])
    ring = []
    for q in range(n):
        ring.append((order[q] * 2, order[(q + 1) % n] * 2))
        ring.append((order[(q + 1) % n] * 2 + 1, order[q] * 2 + 1))
    sign = 1 - 2 * me

    def take(step):
        q = (pos - sign * (1 + step) + 2 * n) % n
        return lax.dynamic_index_in_dim(blocks, owner[q], 0, keepdims=False)

    acc = take(0)
    for step in range(1, n):
        acc = lax.ppermute(acc, (axis, pair), ring) + take(step)
    return acc


def doubling_gather(x, axes):
    size = 1
    for a in axes:
        size *= lax.axis_size(a)
    if size & (size - 1):
        return lax.all_gather(x, axes, axis=0, tiled=True)
    k = size // 2
    while k:
        other = lax.ppermute(x, axes, [(i, i ^ k) for i in range(size)])
        x = jnp.concatenate([x, other], axis=0)
        k //= 2
    return x


def local(images, out_grads, in_signs, out_signs):
    samples = images.shape[0]
    in_part, out_part = project(images, out_grads, in_signs, out_signs)
    width_in = in_part.shape[1]
    cells = in_part.shape[2]
    both = jnp.concatenate([jnp.transpose(in_part, (2, 1, 0)), jnp.transpose(out_part, (2, 1, 0))], axis=1)
    both = both.reshape(-1, samples).T
    both = ring_reduce_scatter(both, "chan", "samp")
    both = jnp.transpose(both.reshape(both.shape[0], cells, -1), (0, 2, 1))
    in_sum = both[:, :width_in]
    out_sum = both[:, width_in:]
    own = sketch(in_sum, out_sum, C)
    every = doubling_gather(own, ("chan", "samp"))
    batch_total = samples * lax.axis_size("samp")
    width = every.shape[1]
    r_rows = damped_cholesky(every, 1.0 / batch_total, lax.axis_index("chan"), lax.axis_size("chan"))
    return (own[None], r_rows)


def solution(mesh):
    in_specs = (
        P(("parts", "samp"), "chan", None),
        P(("parts", "samp"), "chan", None),
        P("chan", None),
        P("chan", None),
    )
    out_specs = (P("samp", ("parts", "chan"), None), P(("parts", "chan"), None))
    return jax.shard_map(local, mesh=mesh, in_specs=in_specs, out_specs=out_specs, check_vma=False)
```

```python
import math

import jax
import jax.numpy as jnp
from jax import lax
from jax.experimental import pallas as pl
from jax.experimental.pallas import tpu as pltpu
from jax.sharding import PartitionSpec as P
import functools

C = 256
HI = lax.Precision.HIGHEST


def _factor_block(d, b):
    rows = lax.broadcasted_iota(jnp.int32, (b, 2 * b), 0)
    lanes = lax.broadcasted_iota(jnp.int32, (1, 2 * b), 1)
    x = jnp.concatenate([d, jnp.eye(b, dtype=jnp.float32)], axis=1)
    for j in range(b):
        row = x[j:j + 1, :]
        s = lax.rsqrt(row[:, j:j + 1])
        r = jnp.where(lanes >= j, row * s, 0.0)
        c = jnp.where(rows[:, :1] > j, x[:, j:j + 1] * s, 0.0)
        x = jnp.where(rows == j, r, x - c * r)
    return x[:, :b], x[:, b:]


def _chol_kernel(f_ref, c_ref, o_ref, w_ref, r_ref, *, nb, b, scale):
    n = nb * b
    f = f_ref[...]
    eye = jnp.eye(b, dtype=jnp.float32)
    for i in range(nb):
        g = lax.dot_general(f[:, i * b:(i + 1) * b], f, (((0,), (0,)), ((), ())), precision=HI,
                            preferred_element_type=jnp.float32) * scale
        w_ref[i] = g
        w_ref[i, :, i * b:(i + 1) * b] = g[:, i * b:(i + 1) * b] + eye

    def diag(k):
        wk = w_ref[k]
        d = jnp.zeros((b, b), jnp.float32)
        for j in range(nb):
            d = jnp.where(k == j, wk[:, j * b:(j + 1) * b], d)
        return d

    def panel(k, rkk, linv):
        pfull = jnp.dot(linv, w_ref[k], precision=HI, preferred_element_type=jnp.float32)
        blocks = []
        pblocks = []
        for j in range(nb):
            pj = pfull[:, j * b:(j + 1) * b]
            blocks.append(jnp.where(j > k, pj, jnp.where(j == k, rkk, 0.0)))
            pblocks.append(jnp.where(j > k, pj, 0.0))
        r_ref[pl.ds(pl.multiple_of(k * b, b), b), :] = jnp.concatenate(blocks, axis=1)
        return pblocks

    def step(k, carry):
        rkk, linv = carry
        k1 = k + 1
        wk = w_ref[k]
        a1 = jnp.zeros((b, b), jnp.float32)
        for j in range(nb):
            a1 = jnp.where(k1 == j, wk[:, j * b:(j + 1) * b], a1)
        t1 = jnp.dot(linv, a1, precision=HI, preferred_element_type=jnp.float32)
        d1 = diag(k1) - lax.dot_general(t1, t1, (((0,), (0,)), ((), ())), precision=HI,
                                        preferred_element_type=jnp.float32)
        nxt = _factor_block(d1, b)
        pblocks = panel(k, rkk, linv)
        p = jnp.concatenate(pblocks, axis=1)
        for i in range(1, nb):
            ti = jnp.where(i > k, pblocks[i], 0.0)
            upd = lax.dot_general(ti, p[:, i * b:], (((0,), (0,)), ((), ())), precision=HI,
                                  preferred_element_type=jnp.float32)
            w_ref[i, :, i * b:] = w_ref[i, :, i * b:] - upd
        return nxt

    last = lax.fori_loop(0, nb - 1, step, _factor_block(diag(0), b))
    panel(nb - 1, *last)
    rows = o_ref.shape[0]
    o_ref[...] = r_ref[pl.ds(pl.multiple_of(c_ref[0] * rows, 8), rows), :]


def damped_cholesky(f, scale, part, parts, b=128, interpret=False):
    n = f.shape[1]
    nb = n // b
    rows = n // parts
    return pl.pallas_call(
        functools.partial(_chol_kernel, nb=nb, b=b, scale=scale),
        out_shape=jax.ShapeDtypeStruct((rows, n), jnp.float32),
        in_specs=[pl.BlockSpec(memory_space=pltpu.VMEM), pl.BlockSpec(memory_space=pltpu.SMEM)],
        out_specs=pl.BlockSpec(memory_space=pltpu.VMEM),
        scratch_shapes=[pltpu.VMEM((nb, b, n), jnp.float32), pltpu.VMEM((n, n), jnp.float32)],
        compiler_params=pltpu.CompilerParams(vmem_limit_bytes=48 * 1024 * 1024),
        interpret=interpret,
    )(f, jnp.reshape(part, (1,)).astype(jnp.int32))


def project(images, out_grads, in_signs, out_signs):
    samples, channels, cells = images.shape
    side_in = math.isqrt(cells)
    picture = images.reshape(samples, channels, side_in, side_in)
    width_in = in_signs.shape[1] // 9
    in_matrix = (2 * in_signs - 1).astype(jnp.bfloat16).reshape(channels, 3, 3, width_in)
    kernel = jnp.transpose(in_matrix, (3, 0, 1, 2))
    in_part = lax.conv_general_dilated(
        picture,
        kernel,
        window_strides=(2, 2),
        padding=((1, 1), (1, 1)),
        dimension_numbers=("NCHW", "OIHW", "NCHW"),
        preferred_element_type=jnp.float32,
    )
    in_part = in_part.reshape(samples, width_in, -1)
    out_matrix = (2 * out_signs - 1).astype(jnp.bfloat16)
    out_part = jnp.einsum("ncp,cl->nlp", out_grads, out_matrix, preferred_element_type=jnp.float32)
    return (in_part, out_part)


def sketch(in_sum, out_sum, total_channels):
    in_feat = in_sum / math.sqrt(9 * total_channels)
    out_feat = out_sum / math.sqrt(total_channels)
    cells = in_sum.shape[2]
    outer = jnp.einsum(
        "nlp,njp->nlj", out_feat, in_feat, precision=lax.Precision.HIGHEST
    ) / math.sqrt(cells)
    return outer.reshape(outer.shape[0], -1)


def _ring_order(n):
    if n % 2:
        return list(range(n))
    return list(range(0, n, 2)) + list(range(n - 1, 0, -2))


def ring_reduce_scatter(x, axis, pair):
    n = lax.axis_size(axis)
    order = _ring_order(n)
    me = lax.axis_index(pair)
    pos = jnp.asarray([order.index(c) for c in range(n)], jnp.int32)[lax.axis_index(axis)]
    owner = jnp.asarray(order, jnp.int32)
    blocks = x.reshape(n, -1, x.shape[-1])
    ring = []
    for q in range(n):
        ring.append((order[q] * 2, order[(q + 1) % n] * 2))
        ring.append((order[(q + 1) % n] * 2 + 1, order[q] * 2 + 1))
    sign = 1 - 2 * me

    def take(step):
        q = (pos - sign * (1 + step) + 2 * n) % n
        return lax.dynamic_index_in_dim(blocks, owner[q], 0, keepdims=False)

    acc = take(0)
    for step in range(1, n):
        acc = lax.ppermute(acc, (axis, pair), ring) + take(step)
    return acc


def doubling_gather(x, axes):
    size = 1
    for a in axes:
        size *= lax.axis_size(a)
    if size & (size - 1):
        return lax.all_gather(x, axes, axis=0, tiled=True)
    k = size // 2
    while k:
        other = lax.ppermute(x, axes, [(i, i ^ k) for i in range(size)])
        x = jnp.concatenate([x, other], axis=0)
        k //= 2
    return x


def local(images, out_grads, in_signs, out_signs):
    samples = images.shape[0]
    in_part, out_part = project(images, out_grads, in_signs, out_signs)
    width_in = in_part.shape[1]
    cells = in_part.shape[2]
    both = jnp.concatenate([jnp.transpose(in_part, (2, 1, 0)), jnp.transpose(out_part, (2, 1, 0))], axis=1)
    both = both.reshape(-1, samples).T
    both = ring_reduce_scatter(both, "chan", "samp")
    both = jnp.transpose(both.reshape(both.shape[0], cells, -1), (0, 2, 1))
    in_sum = both[:, :width_in]
    out_sum = both[:, width_in:]
    own = sketch(in_sum, out_sum, C)
    every = doubling_gather(own, ("chan", "samp"))
    batch_total = samples * lax.axis_size("samp")
    width = every.shape[1]
    r_rows = damped_cholesky(every, 1.0 / batch_total, lax.axis_index("chan"), lax.axis_size("chan"))
    return (own[None], r_rows)


def solution(mesh):
    in_specs = (
        P(("parts", "samp"), "chan", None),
        P(("parts", "samp"), "chan", None),
        P("chan", None),
        P("chan", None),
    )
    out_specs = (P("samp", ("parts", "chan"), None), P(("parts", "chan"), None))
    return jax.shard_map(local, mesh=mesh, in_specs=in_specs, out_specs=out_specs, check_vma=False)
```

```python
import math

import jax
import jax.numpy as jnp
from jax import lax
from jax.experimental import pallas as pl
from jax.experimental.pallas import tpu as pltpu
from jax.sharding import PartitionSpec as P
import functools

C = 256
HI = lax.Precision.HIGHEST


def _factor_block(d, b):
    rows = lax.broadcasted_iota(jnp.int32, (b, 2 * b), 0)
    lanes = lax.broadcasted_iota(jnp.int32, (1, 2 * b), 1)
    x = jnp.concatenate([d, jnp.eye(b, dtype=jnp.float32)], axis=1)
    for j in range(b):
        row = x[j:j + 1, :]
        s = lax.rsqrt(row[:, j:j + 1])
        r = jnp.where(lanes >= j, row * s, 0.0)
        c = jnp.where(rows[:, :1] > j, x[:, j:j + 1] * s, 0.0)
        x = jnp.where(rows == j, r, x - c * r)
    return x[:, :b], x[:, b:]


def _chol_kernel(f_ref, c_ref, o_ref, w_ref, r_ref, *, nb, b, scale):
    n = nb * b
    f = f_ref[...]
    eye = jnp.eye(b, dtype=jnp.float32)
    for i in range(nb):
        g = lax.dot_general(f[:, i * b:(i + 1) * b], f, (((0,), (0,)), ((), ())), precision=HI,
                            preferred_element_type=jnp.float32) * scale
        w_ref[i] = g
        w_ref[i, :, i * b:(i + 1) * b] = g[:, i * b:(i + 1) * b] + eye

    def diag(k):
        return w_ref[k, :, pl.ds(pl.multiple_of(k * b, b), b)]

    def panel(k, rkk, linv):
        pfull = jnp.dot(linv, w_ref[k], precision=HI, preferred_element_type=jnp.float32)
        blocks = []
        pblocks = []
        for j in range(nb):
            pj = pfull[:, j * b:(j + 1) * b]
            blocks.append(jnp.where(j > k, pj, jnp.where(j == k, rkk, 0.0)))
            pblocks.append(jnp.where(j > k, pj, 0.0))
        r_ref[pl.ds(pl.multiple_of(k * b, b), b), :] = jnp.concatenate(blocks, axis=1)
        return pblocks

    def step(k, carry):
        rkk, linv = carry
        k1 = k + 1
        a1 = w_ref[k, :, pl.ds(pl.multiple_of(k1 * b, b), b)]
        t1 = jnp.dot(linv, a1, precision=HI, preferred_element_type=jnp.float32)
        d1 = diag(k1) - lax.dot_general(t1, t1, (((0,), (0,)), ((), ())), precision=HI,
                                        preferred_element_type=jnp.float32)
        nxt = _factor_block(d1, b)
        pblocks = panel(k, rkk, linv)
        p = jnp.concatenate(pblocks, axis=1)
        for i in range(1, nb):
            ti = jnp.where(i > k, pblocks[i], 0.0)
            upd = lax.dot_general(ti, p[:, i * b:], (((0,), (0,)), ((), ())), precision=HI,
                                  preferred_element_type=jnp.float32)
            w_ref[i, :, i * b:] = w_ref[i, :, i * b:] - upd
        return nxt

    last = lax.fori_loop(0, nb - 1, step, _factor_block(diag(0), b))
    panel(nb - 1, *last)
    rows = o_ref.shape[0]
    o_ref[...] = r_ref[pl.ds(pl.multiple_of(c_ref[0] * rows, 8), rows), :]


def damped_cholesky(f, scale, part, parts, b=128, interpret=False):
    n = f.shape[1]
    nb = n // b
    rows = n // parts
    return pl.pallas_call(
        functools.partial(_chol_kernel, nb=nb, b=b, scale=scale),
        out_shape=jax.ShapeDtypeStruct((rows, n), jnp.float32),
        in_specs=[pl.BlockSpec(memory_space=pltpu.VMEM), pl.BlockSpec(memory_space=pltpu.SMEM)],
        out_specs=pl.BlockSpec(memory_space=pltpu.VMEM),
        scratch_shapes=[pltpu.VMEM((nb, b, n), jnp.float32), pltpu.VMEM((n, n), jnp.float32)],
        compiler_params=pltpu.CompilerParams(vmem_limit_bytes=48 * 1024 * 1024),
        interpret=interpret,
    )(f, jnp.reshape(part, (1,)).astype(jnp.int32))


def project(images, out_grads, in_signs, out_signs):
    samples, channels, cells = images.shape
    side_in = math.isqrt(cells)
    picture = images.reshape(samples, channels, side_in, side_in)
    width_in = in_signs.shape[1] // 9
    in_matrix = (2 * in_signs - 1).astype(jnp.bfloat16).reshape(channels, 3, 3, width_in)
    kernel = jnp.transpose(in_matrix, (3, 0, 1, 2))
    in_part = lax.conv_general_dilated(
        picture,
        kernel,
        window_strides=(2, 2),
        padding=((1, 1), (1, 1)),
        dimension_numbers=("NCHW", "OIHW", "NCHW"),
        preferred_element_type=jnp.float32,
    )
    in_part = in_part.reshape(samples, width_in, -1)
    out_matrix = (2 * out_signs - 1).astype(jnp.bfloat16)
    out_part = jnp.einsum("ncp,cl->nlp", out_grads, out_matrix, preferred_element_type=jnp.float32)
    return (in_part, out_part)


def sketch(in_sum, out_sum, total_channels):
    in_feat = in_sum / math.sqrt(9 * total_channels)
    out_feat = out_sum / math.sqrt(total_channels)
    cells = in_sum.shape[2]
    outer = jnp.einsum(
        "nlp,njp->nlj", out_feat, in_feat, precision=lax.Precision.HIGHEST
    ) / math.sqrt(cells)
    return outer.reshape(outer.shape[0], -1)


def _ring_order(n):
    if n % 2:
        return list(range(n))
    return list(range(0, n, 2)) + list(range(n - 1, 0, -2))


def ring_reduce_scatter(x, axis, pair):
    n = lax.axis_size(axis)
    order = _ring_order(n)
    me = lax.axis_index(pair)
    pos = jnp.asarray([order.index(c) for c in range(n)], jnp.int32)[lax.axis_index(axis)]
    owner = jnp.asarray(order, jnp.int32)
    blocks = x.reshape(n, -1, x.shape[-1])
    ring = []
    for q in range(n):
        ring.append((order[q] * 2, order[(q + 1) % n] * 2))
        ring.append((order[(q + 1) % n] * 2 + 1, order[q] * 2 + 1))
    sign = 1 - 2 * me

    def take(step):
        q = (pos - sign * (1 + step) + 2 * n) % n
        return lax.dynamic_index_in_dim(blocks, owner[q], 0, keepdims=False)

    acc = take(0)
    for step in range(1, n):
        acc = lax.ppermute(acc, (axis, pair), ring) + take(step)
    return acc


def doubling_gather(x, axes):
    size = 1
    for a in axes:
        size *= lax.axis_size(a)
    if size & (size - 1):
        return lax.all_gather(x, axes, axis=0, tiled=True)
    k = size // 2
    while k:
        other = lax.ppermute(x, axes, [(i, i ^ k) for i in range(size)])
        x = jnp.concatenate([x, other], axis=0)
        k //= 2
    return x


def local(images, out_grads, in_signs, out_signs):
    samples = images.shape[0]
    in_part, out_part = project(images, out_grads, in_signs, out_signs)
    width_in = in_part.shape[1]
    cells = in_part.shape[2]
    both = jnp.concatenate([jnp.transpose(in_part, (2, 1, 0)), jnp.transpose(out_part, (2, 1, 0))], axis=1)
    both = both.reshape(-1, samples).T
    both = ring_reduce_scatter(both, "chan", "samp")
    both = jnp.transpose(both.reshape(both.shape[0], cells, -1), (0, 2, 1))
    in_sum = both[:, :width_in]
    out_sum = both[:, width_in:]
    own = sketch(in_sum, out_sum, C)
    every = doubling_gather(own, ("chan", "samp"))
    batch_total = samples * lax.axis_size("samp")
    width = every.shape[1]
    r_rows = damped_cholesky(every, 1.0 / batch_total, lax.axis_index("chan"), lax.axis_size("chan"))
    return (own[None], r_rows)


def solution(mesh):
    in_specs = (
        P(("parts", "samp"), "chan", None),
        P(("parts", "samp"), "chan", None),
        P("chan", None),
        P("chan", None),
    )
    out_specs = (P("samp", ("parts", "chan"), None), P(("parts", "chan"), None))
    return jax.shard_map(local, mesh=mesh, in_specs=in_specs, out_specs=out_specs, check_vma=False)
```

```python
import math

import jax
import jax.numpy as jnp
from jax import lax
from jax.experimental import pallas as pl
from jax.experimental.pallas import tpu as pltpu
from jax.sharding import PartitionSpec as P
import functools

C = 256
HI = lax.Precision.HIGHEST


def _factor_block(d, b):
    rows = lax.broadcasted_iota(jnp.int32, (b, 2 * b), 0)
    lanes = lax.broadcasted_iota(jnp.int32, (1, 2 * b), 1)
    x = jnp.concatenate([d, jnp.eye(b, dtype=jnp.float32)], axis=1)
    for j in range(b):
        row = x[j:j + 1, :]
        s = lax.rsqrt(row[:, j:j + 1])
        r = jnp.where(lanes >= j, row * s, 0.0)
        c = jnp.where(rows[:, :1] > j, x[:, j:j + 1] * s, 0.0)
        x = jnp.where(rows == j, r, x - c * r)
    return x[:, :b], x[:, b:]


def _chol_kernel(f_ref, c_ref, o_ref, w_ref, r_ref, *, nb, b, scale):
    n = nb * b
    f = f_ref[...]
    eye = jnp.eye(b, dtype=jnp.float32)
    for i in range(nb):
        g = lax.dot_general(f[:, i * b:(i + 1) * b], f, (((0,), (0,)), ((), ())), precision=HI,
                            preferred_element_type=jnp.float32) * scale
        w_ref[i] = g
        w_ref[i, :, i * b:(i + 1) * b] = g[:, i * b:(i + 1) * b] + eye

    def diag(k):
        wk = w_ref[k]
        d = jnp.zeros((b, b), jnp.float32)
        for j in range(nb):
            d = jnp.where(k == j, wk[:, j * b:(j + 1) * b], d)
        return d

    def panel(k, rkk, linv):
        pfull = jnp.dot(linv, w_ref[k], precision=HI, preferred_element_type=jnp.float32)
        blocks = []
        pblocks = []
        for j in range(nb):
            pj = pfull[:, j * b:(j + 1) * b]
            blocks.append(jnp.where(j > k, pj, jnp.where(j == k, rkk, 0.0)))
            pblocks.append(jnp.where(j > k, pj, 0.0))
        r_ref[pl.ds(pl.multiple_of(k * b, b), b), :] = jnp.concatenate(blocks, axis=1)
        return pblocks

    def step(k, carry):
        rkk, linv = carry
        k1 = k + 1
        wk = w_ref[k]
        a1 = jnp.zeros((b, b), jnp.float32)
        for j in range(nb):
            a1 = jnp.where(k1 == j, wk[:, j * b:(j + 1) * b], a1)
        t1 = jnp.dot(linv, a1, precision=HI, preferred_element_type=jnp.float32)
        d1 = diag(k1) - lax.dot_general(t1, t1, (((0,), (0,)), ((), ())), precision=HI,
                                        preferred_element_type=jnp.float32)
        nxt = _factor_block(d1, b)
        pblocks = panel(k, rkk, linv)
        p = jnp.concatenate(pblocks, axis=1)
        for i in range(1, nb):
            ti = jnp.where(i > k, pblocks[i], 0.0)
            upd = lax.dot_general(ti, p[:, i * b:], (((0,), (0,)), ((), ())), precision=HI,
                                  preferred_element_type=jnp.float32)
            w_ref[i, :, i * b:] = w_ref[i, :, i * b:] - upd
        return nxt

    last = lax.fori_loop(0, nb - 1, step, _factor_block(diag(0), b))
    panel(nb - 1, *last)
    rows = o_ref.shape[0]
    o_ref[...] = r_ref[pl.ds(pl.multiple_of(c_ref[0] * rows, 8), rows), :]


def damped_cholesky(f, scale, part, parts, b=128, interpret=False):
    n = f.shape[1]
    nb = n // b
    rows = n // parts
    return pl.pallas_call(
        functools.partial(_chol_kernel, nb=nb, b=b, scale=scale),
        out_shape=jax.ShapeDtypeStruct((rows, n), jnp.float32),
        in_specs=[pl.BlockSpec(memory_space=pltpu.VMEM), pl.BlockSpec(memory_space=pltpu.SMEM)],
        out_specs=pl.BlockSpec(memory_space=pltpu.VMEM),
        scratch_shapes=[pltpu.VMEM((nb, b, n), jnp.float32), pltpu.VMEM((n, n), jnp.float32)],
        compiler_params=pltpu.CompilerParams(vmem_limit_bytes=48 * 1024 * 1024),
        interpret=interpret,
    )(f, jnp.reshape(part, (1,)).astype(jnp.int32))


def project(images, out_grads, in_signs, out_signs):
    samples, channels, cells = images.shape
    side_in = math.isqrt(cells)
    picture = images.reshape(samples, channels, side_in, side_in)
    width_in = in_signs.shape[1] // 9
    in_matrix = (2 * in_signs - 1).astype(jnp.bfloat16).reshape(channels, 3, 3, width_in)
    kernel = jnp.transpose(in_matrix, (3, 0, 1, 2))
    in_part = lax.conv_general_dilated(
        picture,
        kernel,
        window_strides=(2, 2),
        padding=((1, 1), (1, 1)),
        dimension_numbers=("NCHW", "OIHW", "NCHW"),
        preferred_element_type=jnp.float32,
    )
    in_part = in_part.reshape(samples, width_in, -1)
    out_matrix = (2 * out_signs - 1).astype(jnp.bfloat16)
    out_part = jnp.einsum("ncp,cl->nlp", out_grads, out_matrix, preferred_element_type=jnp.float32)
    return (in_part, out_part)


def sketch(in_sum, out_sum, total_channels):
    in_feat = in_sum / math.sqrt(9 * total_channels)
    out_feat = out_sum / math.sqrt(total_channels)
    cells = in_sum.shape[1]
    outer = jnp.einsum(
        "npl,npj->nlj", out_feat, in_feat, precision=lax.Precision.HIGHEST
    ) / math.sqrt(cells)
    return outer.reshape(outer.shape[0], -1)


def _ring_order(n):
    if n % 2:
        return list(range(n))
    return list(range(0, n, 2)) + list(range(n - 1, 0, -2))


def ring_reduce_scatter(x, axis, pair):
    n = lax.axis_size(axis)
    order = _ring_order(n)
    me = lax.axis_index(pair)
    pos = jnp.asarray([order.index(c) for c in range(n)], jnp.int32)[lax.axis_index(axis)]
    owner = jnp.asarray(order, jnp.int32)
    blocks = x.reshape(n, -1, x.shape[-1])
    ring = []
    for q in range(n):
        ring.append((order[q] * 2, order[(q + 1) % n] * 2))
        ring.append((order[(q + 1) % n] * 2 + 1, order[q] * 2 + 1))
    sign = 1 - 2 * me

    def take(step):
        q = (pos - sign * (1 + step) + 2 * n) % n
        return lax.dynamic_index_in_dim(blocks, owner[q], 0, keepdims=False)

    acc = take(0)
    for step in range(1, n):
        acc = lax.ppermute(acc, (axis, pair), ring) + take(step)
    return acc


def doubling_gather(x, axes):
    size = 1
    for a in axes:
        size *= lax.axis_size(a)
    if size & (size - 1):
        return lax.all_gather(x, axes, axis=0, tiled=True)
    k = size // 2
    while k:
        other = lax.ppermute(x, axes, [(i, i ^ k) for i in range(size)])
        x = jnp.concatenate([x, other], axis=0)
        k //= 2
    return x


def local(images, out_grads, in_signs, out_signs):
    samples = images.shape[0]
    in_part, out_part = project(images, out_grads, in_signs, out_signs)
    width_in = in_part.shape[1]
    cells = in_part.shape[2]
    both = jnp.concatenate([jnp.transpose(in_part, (2, 1, 0)), jnp.transpose(out_part, (2, 1, 0))], axis=1)
    both = both.reshape(-1, samples).T
    both = ring_reduce_scatter(both, "chan", "samp")
    both = both.reshape(both.shape[0], cells, -1)
    in_sum = both[:, :, :width_in]
    out_sum = both[:, :, width_in:]
    own = sketch(in_sum, out_sum, C)
    every = doubling_gather(own, ("chan", "samp"))
    batch_total = samples * lax.axis_size("samp")
    width = every.shape[1]
    r_rows = damped_cholesky(every, 1.0 / batch_total, lax.axis_index("chan"), lax.axis_size("chan"))
    return (own[None], r_rows)


def solution(mesh):
    in_specs = (
        P(("parts", "samp"), "chan", None),
        P(("parts", "samp"), "chan", None),
        P("chan", None),
        P("chan", None),
    )
    out_specs = (P("samp", ("parts", "chan"), None), P(("parts", "chan"), None))
    return jax.shard_map(local, mesh=mesh, in_specs=in_specs, out_specs=out_specs, check_vma=False)
```
